512 devices in a mesh: region: 8 (over z), dom: 64 (over y, x, core).
Axes of the slice: x: 4, y: 8, z: 8, core: 2. Of those that a mesh axis runs over, the one named last changes fastest.
Arguments:
- gauges: bfloat16 [524288, 384], P(('region', 'dom')), may hold values from -24 to 24
- couplings: bfloat16 [4096, 3, 128, 128], P(('region', 'dom')), may hold values from -0.3125 to 0.3125
- adjacency: int32 [4096, 3], P(('region', 'dom')), may hold values from 0 to 15
- send_list: int32 [1024], P(('region', 'dom')), may hold values from 0 to 7
- coverage: int32 [4096, 2], P(('region', 'dom')), may hold values from 0 to 4
- positive: int32 [524288], P(('region', 'dom')), may hold values from 0 to 255
- patches: bfloat16 [65536, 512], P(('region', 'dom')), may hold values from -24 to 24
- message_weight: bfloat16 [384, 384], replicated, may hold values from -0.3125 to 0.3125
- self_weight: bfloat16 [384, 384], replicated, may hold values from -0.3125 to 0.3125
- output_weight: bfloat16 [384, 512], replicated, may hold values from -0.3125 to 0.3125
- patch_weight: bfloat16 [512, 512], replicated, may hold values from -0.25 to 0.25
Outputs:
- grad_message: bfloat16 [384, 384], P('dom')
- grad_self: bfloat16 [384, 384], P('dom')
- grad_output: bfloat16 [384, 512], P('dom')
- grad_patch: bfloat16 [512, 512], P('dom')
The draws below stay inside these ranges and needn't reach their ends.
Inputs may be any that keep to these rules, and one draw needn't show every extreme that they name: `adjacency`: indexes the partition's block table of 16 entries. `send_list`: indexes the partition's own blocks. `coverage`: indexes the partition's patch table of 5 entries.
All inputs are finite; a program needn't handle non-finite values.
Results may differ from the reference program's by a relative error of at most 0.015.
Values may be sent and summed in bfloat16 or wider, within the bound.
No kernel may reach another device: no remote copies, remote signals or barrier semaphores. Data moves between devices by JAX's collectives and lax.ppermute only.
A program may use at most 64 MiB of HBM per device.

```python
import math
import jax
import jax.numpy as jnp
from jax import lax

D = 384
E = 512
BLOCK = 128
BLOCKS_DEV = 8
HOOD = 3
SEND = 2
PATCH_DEV = 1
COVER = 2
GAUGES = 524288
BLOCKS = 4096
PATCHES = 65536
SENDS = 1024
N_REGION = 8
N_DOM = 64


def place_ends(result, rng, least, high):
    longest = result.shape.index(max(result.shape))
    spots = []
    for shift in (0, 1):
        where = [jax.random.randint(jax.random.fold_in(rng, axis), (), 0, length) for axis, length in enumerate(result.shape)]
        where[longest] = (where[longest] + shift) % result.shape[longest]
        spots.append(tuple(where))
    return result.at[spots[0]].set(least).at[spots[1]].set(high)


def with_spikes(values, rng, source, target, parts, factor):
    owner, partner = [(jnp.arange(values.shape[position]) // (values.shape[position] // parts)).reshape([-1 if axis == position else 1 for axis in range(values.ndim)]) for position in (source, target)]
    chosen = jax.random.permutation(rng, parts)[partner]
    strong = (owner == chosen) | (owner == (partner + parts // 2) % parts)
    return jnp.where(strong, factor * values, values)


def levels(stream_key, extent, cuts, low, largest):
    factor_of = 1.0
    for position, blocks in cuts:
        heights = jax.random.uniform(jax.random.fold_in(jax.random.fold_in(stream_key, 6), position), (blocks,), jnp.float32, low / len(cuts), largest / len(cuts))
        factor_of = factor_of * jnp.repeat(jnp.exp(heights), extent[position] // blocks).reshape((-1,) + (1,) * (len(extent) - 1 - position))
    return factor_of


def bell_draw(key, dims, scale, reach, cuts=(), held_as=jnp.bfloat16):
    values = jax.random.normal(key, dims, jnp.float32) * scale
    if len(cuts) > 0:
        values = levels(key, dims, cuts, -0.22, 0.18) * values
    return jnp.clip(values, min=-reach, max=reach).astype(held_as)


def heavy_noise(own_key, dims, scale, reach, pieces, heavy, kind=jnp.bfloat16):
    result = scale * jax.random.normal(own_key, dims, jnp.float32)
    if pieces:
        result = result * levels(own_key, dims, pieces, -0.22, 0.18)
    return jnp.clip(with_spikes(result, jax.random.fold_in(own_key, 3), *heavy), -reach, reach).astype(kind)


def setup_inputs(seed: int = 0) -> dict:
    keys = jax.random.split(jax.random.key(seed), 12)
    gauges = heavy_noise(keys[0], (GAUGES, D), 1.0, 24.0, ((0, 512),), (0, 1, 128, 5.5))
    couplings = bell_draw(keys[1], (BLOCKS, HOOD, BLOCK, BLOCK), (BLOCK * HOOD) ** -0.5, 0.3125, ((0, 512),))
    adjacency = place_ends(jax.random.randint(keys[2], (BLOCKS, HOOD), 0, BLOCKS_DEV + 4 * SEND), jax.random.fold_in(keys[2], 1), 0, (BLOCKS_DEV + 4 * SEND) - 1).astype(jnp.int32)
    send_list = place_ends(jax.random.randint(keys[3], (SENDS,), 0, BLOCKS_DEV), jax.random.fold_in(keys[3], 1), 0, BLOCKS_DEV - 1).astype(jnp.int32)
    coverage = place_ends(jax.random.randint(keys[4], (BLOCKS, COVER), 0, 5 * PATCH_DEV), jax.random.fold_in(keys[4], 1), 0, (5 * PATCH_DEV) - 1).astype(jnp.int32)
    positive = place_ends(jax.random.randint(keys[5], (GAUGES,), 0, COVER * BLOCK), jax.random.fold_in(keys[5], 1), 0, (COVER * BLOCK) - 1).astype(jnp.int32)
    patches = heavy_noise(keys[6], (PATCHES, E), 1.0, 24.0, ((0, 512),), (0, 1, 512, 6.0))
    message_weight = bell_draw(keys[7], (D, D), D ** -0.5, 0.3125)
    self_weight = bell_draw(keys[8], (D, D), D ** -0.5, 0.3125)
    output_weight = bell_draw(keys[9], (D, E), D ** -0.5, 0.3125)
    patch_weight = bell_draw(keys[10], (E, E), E ** -0.5, 0.25)
    return {"gauges": gauges, "couplings": couplings, "adjacency": adjacency, "send_list": send_list, "coverage": coverage, "positive": positive, "patches": patches, "message_weight": message_weight, "self_weight": self_weight, "output_weight": output_weight, "patch_weight": patch_weight}


loss_gain = 16.0

def silu_slope(argument):
    sigmoid_v = jax.nn.sigmoid(argument)
    return sigmoid_v * (1.0 + argument * (1.0 - sigmoid_v))

def device_terms(own_blocks, block_table, couplings, adjacency, patch_table, coverage, positive, message_weight, self_weight, output_weight, patch_weight):
    f32 = jnp.float32
    bf16 = jnp.bfloat16
    picked = block_table[adjacency]
    message = jnp.einsum('bkij,bkjd->bid', couplings.astype(f32), picked.astype(f32)).astype(bf16).reshape(-1, D)
    gauge_rows = own_blocks.reshape(-1, D)
    pre_act = jnp.dot(message, message_weight, preferred_element_type=f32) + jnp.dot(gauge_rows, self_weight, preferred_element_type=f32)
    hidden = (gauge_rows.astype(f32) + jax.nn.silu(pre_act)).astype(bf16)
    queries = jnp.dot(hidden, output_weight, preferred_element_type=f32).astype(bf16)
    covered = patch_table[coverage]
    flat_cover = covered.reshape(-1, E)
    key_rows = jnp.dot(flat_cover, patch_weight, preferred_element_type=f32).astype(bf16).reshape(BLOCKS_DEV, COVER * BLOCK, E)
    query_blocks = queries.reshape(BLOCKS_DEV, BLOCK, E)
    inv_root = 1.0 / math.sqrt(E)
    logits = jnp.einsum('bie,bje->bij', query_blocks.astype(f32), key_rows.astype(f32)) * inv_root
    soft = jax.nn.softmax(logits, axis=-1)
    columns = jnp.arange(COVER * BLOCK, dtype=jnp.int32)
    target = (positive.reshape(BLOCKS_DEV, BLOCK)[:, :, None] == columns).astype(f32)
    loss_scale = loss_gain / math.sqrt(GAUGES)
    logit_grad = ((soft - target) * loss_scale).astype(bf16)
    query_grad = (jnp.einsum('bij,bje->bie', logit_grad.astype(f32), key_rows.astype(f32)) * inv_root).astype(bf16).reshape(-1, E)
    key_grad = (jnp.einsum('bij,bie->bje', logit_grad.astype(f32), query_blocks.astype(f32)) * inv_root).astype(bf16).reshape(-1, E)
    grad_patch = jnp.dot(flat_cover.T, key_grad, preferred_element_type=f32)
    grad_output = jnp.dot(hidden.T, query_grad, preferred_element_type=f32)
    hidden_grad = jnp.dot(query_grad, output_weight.T, preferred_element_type=f32)
    act_grad = (hidden_grad * silu_slope(pre_act)).astype(bf16)
    grad_message = jnp.dot(message.T, act_grad, preferred_element_type=f32)
    grad_self = jnp.dot(gauge_rows.T, act_grad, preferred_element_type=f32)
    return (grad_message, grad_self, grad_output, grad_patch)

def reference(gauges, couplings, adjacency, send_list, coverage, positive, patches, message_weight, self_weight, output_weight, patch_weight):
    all_blocks = gauges.reshape(N_REGION, N_DOM, BLOCKS_DEV, BLOCK, D)
    all_sends = send_list.reshape(N_REGION, N_DOM, SEND)
    all_patches = patches.reshape(N_REGION, N_DOM, PATCH_DEV, BLOCK, E)
    all_couplings = couplings.reshape(N_REGION, N_DOM, BLOCKS_DEV, HOOD, BLOCK, BLOCK)
    all_adjacency = adjacency.reshape(N_REGION, N_DOM, BLOCKS_DEV, HOOD)
    all_coverage = coverage.reshape(N_REGION, N_DOM, BLOCKS_DEV, COVER)
    all_positive = positive.reshape(N_REGION, N_DOM, BLOCKS_DEV * BLOCK)

    def accumulate(totals, dev_index):
        region = dev_index // N_DOM
        dom_index = dev_index % N_DOM
        own_blocks = all_blocks[region, dom_index]
        block_parts = [own_blocks]
        patch_parts = [all_patches[region, dom_index]]
        for step_by in (1, 2, -1, -2):
            source = (dom_index - step_by) % N_DOM
            block_parts.append(all_blocks[region, source][all_sends[region, source]])
            patch_parts.append(all_patches[region, source])
        block_table = jnp.concatenate(block_parts, axis=0)
        patch_table = jnp.concatenate(patch_parts, axis=0)
        terms = device_terms(own_blocks, block_table, all_couplings[region, dom_index], all_adjacency[region, dom_index], patch_table, all_coverage[region, dom_index], all_positive[region, dom_index], message_weight, self_weight, output_weight, patch_weight)
        return (tuple((total + term for total, term in zip(totals, terms))), None)
    start = (jnp.zeros((D, D), jnp.float32), jnp.zeros((D, D), jnp.float32), jnp.zeros((D, E), jnp.float32), jnp.zeros((E, E), jnp.float32))
    totals, _ = lax.scan(accumulate, start, jnp.arange(N_REGION * N_DOM, dtype=jnp.int32))
    return (totals[0].astype(jnp.bfloat16), totals[1].astype(jnp.bfloat16), totals[2].astype(jnp.bfloat16), totals[3].astype(jnp.bfloat16))
```

```python
import math

import jax
import jax.numpy as jnp
from jax import lax
from jax.sharding import PartitionSpec as P

BLOCK = 128


loss_gain = 16.0
offsets_by = (1, 2, -1, -2)
halving_bits = (0, 1, 3, 2, 4, 5)


def passed_along(shard, axis, by):
    count = lax.axis_size(axis)
    return lax.ppermute(shard, axis, [(i, (i + by) % count) for i in range(count)])


def swapped(shard, axis, mask):
    count = lax.axis_size(axis)
    return lax.ppermute(shard, axis, [(i, i ^ mask) for i in range(count)])


def silu_slope(argument):
    sigmoid_v = jax.nn.sigmoid(argument)
    return sigmoid_v * (1.0 + argument * (1.0 - sigmoid_v))


def neighbour_tables(blocks, send_list, patch_blocks):
    outgoing = blocks[send_list]
    n_send = outgoing.shape[0]
    gauge_size = outgoing.size
    packed = jnp.concatenate([outgoing.reshape(-1), patch_blocks.reshape(-1)])
    block_parts = [blocks]
    patch_parts = [patch_blocks]
    for step_by in offsets_by:
        got = passed_along(packed, "dom", step_by)
        block_parts.append(got[:gauge_size].reshape(n_send, BLOCK, blocks.shape[2]))
        patch_parts.append(got[gauge_size:].reshape(patch_blocks.shape))
    return jnp.concatenate(block_parts, axis=0), jnp.concatenate(patch_parts, axis=0)


def reduce_to_share(terms, n_dom):
    flat = jnp.concatenate([t.reshape(n_dom, -1) for t in terms], axis=1)
    n_bits = n_dom.bit_length() - 1
    me = lax.axis_index("dom")
    held = flat.reshape((2,) * n_bits + (flat.shape[1],))
    axes = list(range(n_bits))
    for bit in halving_bits[:n_bits]:
        pos = axes.index(n_bits - 1 - bit)
        mine_bit = (me >> bit) & 1
        mine = lax.dynamic_index_in_dim(held, mine_bit, pos, keepdims=False)
        other = lax.dynamic_index_in_dim(held, 1 - mine_bit, pos, keepdims=False)
        held = mine + swapped(other, "dom", 1 << bit)
        axes.pop(pos)
    share = held.reshape(-1)
    n_region = lax.axis_size("region")
    step = 1
    while step < n_region:
        share = share + swapped(share, "region", step)
        step *= 2
    pieces = []
    start = 0
    for t in terms:
        size = t.size // n_dom
        pieces.append(share[start : start + size].reshape(t.shape[0] // n_dom, t.shape[1]))
        start += size
    return pieces


def shards(
    gauges,
    couplings,
    adjacency,
    send_list,
    coverage,
    positive,
    patches,
    message_weight,
    self_weight,
    output_weight,
    patch_weight,
):
    f32 = jnp.float32
    bf16 = jnp.bfloat16
    width = gauges.shape[1]
    wide = patches.shape[1]
    count = couplings.shape[0]
    blocks = gauges.reshape(count, BLOCK, width)
    patch_blocks = patches.reshape(-1, BLOCK, wide)
    block_table, patch_table = neighbour_tables(blocks, send_list, patch_blocks)
    picked = block_table[adjacency]
    message = (
        jnp.einsum("bkij,bkjd->bid", couplings, picked, preferred_element_type=f32)
        .astype(bf16)
        .reshape(-1, width)
    )
    pre_act = jnp.dot(message, message_weight, preferred_element_type=f32) + jnp.dot(
        gauges, self_weight, preferred_element_type=f32
    )
    hidden = (gauges.astype(f32) + jax.nn.silu(pre_act)).astype(bf16)
    queries = jnp.dot(hidden, output_weight, preferred_element_type=f32).astype(bf16)
    table_keys = (
        jnp.dot(patch_table.reshape(-1, wide), patch_weight, preferred_element_type=f32)
        .astype(bf16)
        .reshape(patch_table.shape)
    )
    key_rows = table_keys[coverage].reshape(count, -1, wide)
    flat_cover = patch_table[coverage].reshape(-1, wide)
    query_blocks = queries.reshape(count, BLOCK, wide)
    inv_root = 1.0 / math.sqrt(wide)
    logits = (
        jnp.einsum("bie,bje->bij", query_blocks, key_rows, preferred_element_type=f32) * inv_root
    )
    soft = jax.nn.softmax(logits, axis=-1)
    columns = jnp.arange(logits.shape[2], dtype=jnp.int32)
    target = (positive.reshape(count, BLOCK)[:, :, None] == columns).astype(f32)
    total_gauges = gauges.shape[0] * lax.axis_size("region") * lax.axis_size("dom")
    loss_scale = loss_gain / math.sqrt(total_gauges)
    logit_grad = ((soft - target) * loss_scale).astype(bf16)
    query_grad = (
        (jnp.einsum("bij,bje->bie", logit_grad, key_rows, preferred_element_type=f32) * inv_root)
        .astype(bf16)
        .reshape(-1, wide)
    )
    key_grad = (
        (
            jnp.einsum("bij,bie->bje", logit_grad, query_blocks, preferred_element_type=f32)
            * inv_root
        )
        .astype(bf16)
        .reshape(-1, wide)
    )
    grad_patch = jnp.dot(flat_cover.T, key_grad, preferred_element_type=f32)
    grad_output = jnp.dot(hidden.T, query_grad, preferred_element_type=f32)
    hidden_grad = jnp.dot(query_grad, output_weight.T, preferred_element_type=f32)
    act_grad = (hidden_grad * silu_slope(pre_act)).astype(bf16)
    grad_message = jnp.dot(message.T, act_grad, preferred_element_type=f32)
    grad_self = jnp.dot(gauges.T, act_grad, preferred_element_type=f32)
    shares = reduce_to_share(
        [grad_message, grad_self, grad_output, grad_patch], lax.axis_size("dom")
    )
    return tuple(s.astype(bf16) for s in shares)


def solution(mesh):
    placed = (
        P(("region", "dom"), None),
        P(("region", "dom"), None, None, None),
        P(("region", "dom"), None),
        P(("region", "dom")),
        P(("region", "dom"), None),
        P(("region", "dom")),
        P(("region", "dom"), None),
        P(),
        P(),
        P(),
        P(),
    )
    return jax.shard_map(
        shards,
        mesh=mesh,
        in_specs=placed,
        out_specs=(P("dom", None), P("dom", None), P("dom", None), P("dom", None)),
        check_vma=False,
    )
```

```python
import math

import jax
import jax.numpy as jnp
from jax import lax
from jax.sharding import PartitionSpec as P

BLOCK = 128


loss_gain = 16.0
offsets_by = (1, 2, -1, -2)


def passed_along(shard, axis, by):
    count = lax.axis_size(axis)
    return lax.ppermute(shard, axis, [(i, (i + by) % count) for i in range(count)])


def swapped(shard, axis, mask):
    count = lax.axis_size(axis)
    return lax.ppermute(shard, axis, [(i, i ^ mask) for i in range(count)])


def silu_slope(argument):
    sigmoid_v = jax.nn.sigmoid(argument)
    return sigmoid_v * (1.0 + argument * (1.0 - sigmoid_v))


def neighbour_tables(blocks, send_list, patch_blocks):
    outgoing = blocks[send_list]
    n_send = outgoing.shape[0]
    gauge_size = outgoing.size
    packed = jnp.concatenate([outgoing.reshape(-1), patch_blocks.reshape(-1)])
    block_parts = [blocks]
    patch_parts = [patch_blocks]
    for step_by in offsets_by:
        got = passed_along(packed, "dom", step_by)
        block_parts.append(got[:gauge_size].reshape(n_send, BLOCK, blocks.shape[2]))
        patch_parts.append(got[gauge_size:].reshape(patch_blocks.shape))
    return jnp.concatenate(block_parts, axis=0), jnp.concatenate(patch_parts, axis=0)


def logical_pairs(n_y, n_x, axis_is_x, mask):
    pairs = []
    for y in range(n_y):
        for x in range(n_x):
            for c in range(2):
                lx, ly = (x - c) % n_x, (y - c) % n_y
                if axis_is_x:
                    lx ^= mask
                else:
                    ly ^= mask
                px, py = (lx + c) % n_x, (ly + c) % n_y
                pairs.append(((y * n_x + x) * 2 + c, (py * n_x + px) * 2 + c))
    return pairs


def reduce_to_share(terms, n_dom, n_x):
    bf16 = jnp.bfloat16
    f32 = jnp.float32
    n_y = n_dom // (2 * n_x)
    flat = jnp.concatenate([t.reshape(n_dom, -1) for t in terms], axis=1)
    width = flat.shape[1]
    me = lax.axis_index("dom")
    core = me % 2
    grid = flat.reshape(n_y, n_x, 2, width)
    mine = lax.dynamic_index_in_dim(grid, core, 2, keepdims=False)
    other = lax.dynamic_index_in_dim(grid, 1 - core, 2, keepdims=False)
    held = mine + swapped(other, "dom", 1)
    wrapped = jnp.concatenate([held, held[:1]], axis=0)
    wrapped = jnp.concatenate([wrapped, wrapped[:, :1]], axis=1)
    held = lax.dynamic_slice(wrapped, (core, core, 0), (n_y, n_x, width))
    lx = (me // 2 % n_x - core) % n_x
    ly = (me // (2 * n_x) - core) % n_y
    x_bits = n_x.bit_length() - 1
    y_bits = n_y.bit_length() - 1
    held = held.reshape((2,) * y_bits + (2,) * x_bits + (width,))
    names = ["y%d" % b for b in reversed(range(y_bits))] + ["x%d" % b for b in reversed(range(x_bits))]
    order = []
    for b in range(max(x_bits, y_bits)):
        if b < x_bits:
            order.append(("x", b))
        if b < y_bits:
            order.append(("y", b))
    for step, (kind, b) in enumerate(order):
        pos = names.index("%s%d" % (kind, b))
        coord = lx if kind == "x" else ly
        mine_bit = (coord >> b) & 1
        mine = lax.dynamic_index_in_dim(held, mine_bit, pos, keepdims=False)
        other = lax.dynamic_index_in_dim(held, 1 - mine_bit, pos, keepdims=False)
        pairs = logical_pairs(n_y, n_x, kind == "x", 1 << b)
        if step < 2:
            got = lax.ppermute(other.astype(bf16), "dom", pairs).astype(f32)
        else:
            got = lax.ppermute(other, "dom", pairs)
        held = mine + got
        names.pop(pos)
    share = held.reshape(-1)
    n_region = lax.axis_size("region")
    region = lax.axis_index("region")
    gathered = [share] + [passed_along(share, "region", k) for k in range(1, n_region)]
    stacked = jnp.stack(gathered)
    ordered = jnp.take(stacked, (region - jnp.arange(n_region)) % n_region, axis=0)
    share = jnp.sum(ordered, axis=0)
    pieces = []
    start = 0
    for t in terms:
        size = t.size // n_dom
        pieces.append(share[start : start + size].reshape(t.shape[0] // n_dom, t.shape[1]))
        start += size
    return pieces


def shards(
    gauges,
    couplings,
    adjacency,
    send_list,
    coverage,
    positive,
    patches,
    message_weight,
    self_weight,
    output_weight,
    patch_weight,
):
    f32 = jnp.float32
    bf16 = jnp.bfloat16
    width = gauges.shape[1]
    wide = patches.shape[1]
    count = couplings.shape[0]
    blocks = gauges.reshape(count, BLOCK, width)
    patch_blocks = patches.reshape(-1, BLOCK, wide)
    block_table, patch_table = neighbour_tables(blocks, send_list, patch_blocks)
    picked = block_table[adjacency]
    message = (
        jnp.einsum("bkij,bkjd->bid", couplings, picked, preferred_element_type=f32)
        .astype(bf16)
        .reshape(-1, width)
    )
    pre_act = jnp.dot(message, message_weight, preferred_element_type=f32) + jnp.dot(
        gauges, self_weight, preferred_element_type=f32
    )
    hidden = (gauges.astype(f32) + jax.nn.silu(pre_act)).astype(bf16)
    queries = jnp.dot(hidden, output_weight, preferred_element_type=f32).astype(bf16)
    table_keys = (
        jnp.dot(patch_table.reshape(-1, wide), patch_weight, preferred_element_type=f32)
        .astype(bf16)
        .reshape(patch_table.shape)
    )
    key_rows = table_keys[coverage].reshape(count, -1, wide)
    flat_cover = patch_table[coverage].reshape(-1, wide)
    query_blocks = queries.reshape(count, BLOCK, wide)
    inv_root = 1.0 / math.sqrt(wide)
    logits = (
        jnp.einsum("bie,bje->bij", query_blocks, key_rows, preferred_element_type=f32) * inv_root
    )
    soft = jax.nn.softmax(logits, axis=-1)
    columns = jnp.arange(logits.shape[2], dtype=jnp.int32)
    target = (positive.reshape(count, BLOCK)[:, :, None] == columns).astype(f32)
    total_gauges = gauges.shape[0] * lax.axis_size("region") * lax.axis_size("dom")
    loss_scale = loss_gain / math.sqrt(total_gauges)
    logit_grad = ((soft - target) * loss_scale).astype(bf16)
    query_grad = (
        (jnp.einsum("bij,bje->bie", logit_grad, key_rows, preferred_element_type=f32) * inv_root)
        .astype(bf16)
        .reshape(-1, wide)
    )
    key_grad = (
        (
            jnp.einsum("bij,bie->bje", logit_grad, query_blocks, preferred_element_type=f32)
            * inv_root
        )
        .astype(bf16)
        .reshape(-1, wide)
    )
    grad_patch = jnp.dot(flat_cover.T, key_grad, preferred_element_type=f32)
    grad_output = jnp.dot(hidden.T, query_grad, preferred_element_type=f32)
    hidden_grad = jnp.dot(query_grad, output_weight.T, preferred_element_type=f32)
    act_grad = (hidden_grad * silu_slope(pre_act)).astype(bf16)
    grad_message = jnp.dot(message.T, act_grad, preferred_element_type=f32)
    grad_self = jnp.dot(gauges.T, act_grad, preferred_element_type=f32)
    shares = reduce_to_share(
        [grad_message, grad_self, grad_output, grad_patch], lax.axis_size("dom"), 4
    )
    return tuple(s.astype(bf16) for s in shares)


def solution(mesh):
    placed = (
        P(("region", "dom"), None),
        P(("region", "dom"), None, None, None),
        P(("region", "dom"), None),
        P(("region", "dom")),
        P(("region", "dom"), None),
        P(("region", "dom")),
        P(("region", "dom"), None),
        P(),
        P(),
        P(),
        P(),
    )
    return jax.shard_map(
        shards,
        mesh=mesh,
        in_specs=placed,
        out_specs=(P("dom", None), P("dom", None), P("dom", None), P("dom", None)),
        check_vma=False,
    )
```

```python
import functools
import math

import jax
import jax.numpy as jnp
from jax import lax
from jax.sharding import PartitionSpec as P

BLOCK = 128


loss_gain = 16.0
offsets_by = (1, 2, -1, -2)


def passed_along(shard, axis, by):
    count = lax.axis_size(axis)
    return lax.ppermute(shard, axis, [(i, (i + by) % count) for i in range(count)])


def swapped(shard, axis, mask):
    count = lax.axis_size(axis)
    return lax.ppermute(shard, axis, [(i, i ^ mask) for i in range(count)])


def silu_slope(argument):
    sigmoid_v = jax.nn.sigmoid(argument)
    return sigmoid_v * (1.0 + argument * (1.0 - sigmoid_v))


def neighbour_tables(blocks, send_list, patch_blocks):
    outgoing = blocks[send_list]
    n_send = outgoing.shape[0]
    gauge_size = outgoing.size
    packed = jnp.concatenate([outgoing.reshape(-1), patch_blocks.reshape(-1)])
    block_parts = [blocks]
    patch_parts = [patch_blocks]
    for step_by in offsets_by:
        got = passed_along(packed, "dom", step_by)
        block_parts.append(got[:gauge_size].reshape(n_send, BLOCK, blocks.shape[2]))
        patch_parts.append(got[gauge_size:].reshape(patch_blocks.shape))
    return jnp.concatenate(block_parts, axis=0), jnp.concatenate(patch_parts, axis=0)


def logical_pairs(n_y, n_x, axis_is_x, mask):
    pairs = []
    for y in range(n_y):
        for x in range(n_x):
            for c in range(2):
                lx, ly = (x - c) % n_x, (y - c) % n_y
                if axis_is_x:
                    lx ^= mask
                else:
                    ly ^= mask
                px, py = (lx + c) % n_x, (ly + c) % n_y
                pairs.append(((y * n_x + x) * 2 + c, (py * n_x + px) * 2 + c))
    return pairs


def share_order(rows, n_dom, n_x):
    n_y = n_dom // (2 * n_x)
    per = rows // n_dom
    order = []
    for c in range(2):
        for ly in range(n_y):
            for lx in range(n_x):
                d = ((ly + c) % n_y * n_x + (lx + c) % n_x) * 2 + c
                order.extend(range(d * per, (d + 1) * per))
    return jnp.array(order, dtype=jnp.int32)


def reduce_to_share(terms, n_dom, n_x):
    bf16 = jnp.bfloat16
    f32 = jnp.float32
    n_y = n_dom // (2 * n_x)
    flat = jnp.concatenate(
        [t[share_order(t.shape[0], n_dom, n_x)].reshape(2, n_y * n_x, -1) for t in terms], axis=2
    )
    width = flat.shape[2]
    me = lax.axis_index("dom")
    core = me % 2
    mine = lax.dynamic_index_in_dim(flat, core, 0, keepdims=False)
    other = lax.dynamic_index_in_dim(flat, 1 - core, 0, keepdims=False)
    held = mine + swapped(other, "dom", 1)
    lx = (me // 2 % n_x - core) % n_x
    ly = (me // (2 * n_x) - core) % n_y
    x_bits = n_x.bit_length() - 1
    y_bits = n_y.bit_length() - 1
    held = held.reshape((2,) * y_bits + (2,) * x_bits + (width,))
    names = ["y%d" % b for b in reversed(range(y_bits))] + ["x%d" % b for b in reversed(range(x_bits))]
    order = []
    for b in range(max(x_bits, y_bits)):
        if b < x_bits:
            order.append(("x", b))
        if b < y_bits:
            order.append(("y", b))
    for step, (kind, b) in enumerate(order):
        pos = names.index("%s%d" % (kind, b))
        coord = lx if kind == "x" else ly
        mine_bit = (coord >> b) & 1
        mine = lax.dynamic_index_in_dim(held, mine_bit, pos, keepdims=False)
        other = lax.dynamic_index_in_dim(held, 1 - mine_bit, pos, keepdims=False)
        pairs = logical_pairs(n_y, n_x, kind == "x", 1 << b)
        if step < 2:
            got = lax.ppermute(other.astype(bf16), "dom", pairs).astype(f32)
        else:
            got = lax.ppermute(other, "dom", pairs)
        held = mine + got
        names.pop(pos)
    share = held.reshape(-1)
    n_region = lax.axis_size("region")
    step = 1
    while step < n_region:
        share = share + swapped(share, "region", step)
        step *= 2
    pieces = []
    start = 0
    for t in terms:
        size = t.size // n_dom
        pieces.append(share[start : start + size].reshape(t.shape[0] // n_dom, t.shape[1]))
        start += size
    return pieces


def shards(
    n_x,
    gauges,
    couplings,
    adjacency,
    send_list,
    coverage,
    positive,
    patches,
    message_weight,
    self_weight,
    output_weight,
    patch_weight,
):
    f32 = jnp.float32
    bf16 = jnp.bfloat16
    width = gauges.shape[1]
    wide = patches.shape[1]
    count = couplings.shape[0]
    blocks = gauges.reshape(count, BLOCK, width)
    patch_blocks = patches.reshape(-1, BLOCK, wide)
    block_table, patch_table = neighbour_tables(blocks, send_list, patch_blocks)
    picked = block_table[adjacency]
    message = (
        jnp.einsum("bkij,bkjd->bid", couplings, picked, preferred_element_type=f32)
        .astype(bf16)
        .reshape(-1, width)
    )
    pre_act = jnp.dot(message, message_weight, preferred_element_type=f32) + jnp.dot(
        gauges, self_weight, preferred_element_type=f32
    )
    hidden = (gauges.astype(f32) + jax.nn.silu(pre_act)).astype(bf16)
    queries = jnp.dot(hidden, output_weight, preferred_element_type=f32).astype(bf16)
    table_keys = (
        jnp.dot(patch_table.reshape(-1, wide), patch_weight, preferred_element_type=f32)
        .astype(bf16)
        .reshape(patch_table.shape)
    )
    key_rows = table_keys[coverage].reshape(count, -1, wide)
    flat_cover = patch_table[coverage].reshape(-1, wide)
    query_blocks = queries.reshape(count, BLOCK, wide)
    inv_root = 1.0 / math.sqrt(wide)
    logits = (
        jnp.einsum("bie,bje->bij", query_blocks, key_rows, preferred_element_type=f32) * inv_root
    )
    soft = jax.nn.softmax(logits, axis=-1)
    columns = jnp.arange(logits.shape[2], dtype=jnp.int32)
    target = (positive.reshape(count, BLOCK)[:, :, None] == columns).astype(f32)
    total_gauges = gauges.shape[0] * lax.axis_size("region") * lax.axis_size("dom")
    loss_scale = loss_gain / math.sqrt(total_gauges)
    logit_grad = ((soft - target) * loss_scale).astype(bf16)
    query_grad = (
        (jnp.einsum("bij,bje->bie", logit_grad, key_rows, preferred_element_type=f32) * inv_root)
        .astype(bf16)
        .reshape(-1, wide)
    )
    key_grad = (
        (
            jnp.einsum("bij,bie->bje", logit_grad, query_blocks, preferred_element_type=f32)
            * inv_root
        )
        .astype(bf16)
        .reshape(-1, wide)
    )
    grad_patch = jnp.dot(flat_cover.T, key_grad, preferred_element_type=f32)
    grad_output = jnp.dot(hidden.T, query_grad, preferred_element_type=f32)
    hidden_grad = jnp.dot(query_grad, output_weight.T, preferred_element_type=f32)
    act_grad = (hidden_grad * silu_slope(pre_act)).astype(bf16)
    grad_message = jnp.dot(message.T, act_grad, preferred_element_type=f32)
    grad_self = jnp.dot(gauges.T, act_grad, preferred_element_type=f32)
    shares = reduce_to_share(
        [grad_message, grad_self, grad_output, grad_patch], lax.axis_size("dom"), n_x
    )
    return tuple(s.astype(bf16) for s in shares)


def solution(mesh):
    placed = (
        P(("region", "dom"), None),
        P(("region", "dom"), None, None, None),
        P(("region", "dom"), None),
        P(("region", "dom")),
        P(("region", "dom"), None),
        P(("region", "dom")),
        P(("region", "dom"), None),
        P(),
        P(),
        P(),
        P(),
    )
    n_x = len({device.coords[0] for device in mesh.devices.flat})
    return jax.shard_map(
        functools.partial(shards, n_x),
        mesh=mesh,
        in_specs=placed,
        out_specs=(P("dom", None), P("dom", None), P("dom", None), P("dom", None)),
        check_vma=False,
    )
```

```python
import functools
import math

import jax
import jax.numpy as jnp
from jax import lax
from jax.sharding import PartitionSpec as P

BLOCK = 128


loss_gain = 16.0
offsets_by = (1, 2, -1, -2)


def passed_along(shard, axis, by):
    count = lax.axis_size(axis)
    return lax.ppermute(shard, axis, [(i, (i + by) % count) for i in range(count)])


def swapped(shard, axis, mask):
    count = lax.axis_size(axis)
    return lax.ppermute(shard, axis, [(i, i ^ mask) for i in range(count)])


def silu_slope(argument):
    sigmoid_v = jax.nn.sigmoid(argument)
    return sigmoid_v * (1.0 + argument * (1.0 - sigmoid_v))


def neighbour_tables(blocks, send_list, patch_blocks):
    outgoing = blocks[send_list]
    n_send = outgoing.shape[0]
    gauge_size = outgoing.size
    packed = jnp.concatenate([outgoing.reshape(-1), patch_blocks.reshape(-1)])
    block_parts = [blocks]
    patch_parts = [patch_blocks]
    for step_by in offsets_by:
        got = passed_along(packed, "dom", step_by)
        block_parts.append(got[:gauge_size].reshape(n_send, BLOCK, blocks.shape[2]))
        patch_parts.append(got[gauge_size:].reshape(patch_blocks.shape))
    return jnp.concatenate(block_parts, axis=0), jnp.concatenate(patch_parts, axis=0)


def logical_pairs(n_y, n_x, axis_is_x, mask):
    pairs = []
    for y in range(n_y):
        for x in range(n_x):
            for c in range(2):
                lx, ly = (x - c) % n_x, (y - c) % n_y
                if axis_is_x:
                    lx ^= mask
                else:
                    ly ^= mask
                px, py = (lx + c) % n_x, (ly + c) % n_y
                pairs.append(((y * n_x + x) * 2 + c, (py * n_x + px) * 2 + c))
    return pairs


def reduce_to_share(terms, n_dom, n_x):
    bf16 = jnp.bfloat16
    f32 = jnp.float32
    n_y = n_dom // (2 * n_x)
    halves = []
    for t in terms:
        grid = t.reshape(n_y, n_x, 2, -1)
        first = grid[:, :, 0]
        second = jnp.roll(grid[:, :, 1], (-1, -1), axis=(0, 1))
        halves.append(jnp.stack([first, second]).reshape(2, n_y * n_x, -1))
    flat = jnp.concatenate(halves, axis=2)
    width = flat.shape[2]
    me = lax.axis_index("dom")
    core = me % 2
    mine = lax.dynamic_index_in_dim(flat, core, 0, keepdims=False)
    other = lax.dynamic_index_in_dim(flat, 1 - core, 0, keepdims=False)
    held = mine + swapped(other, "dom", 1)
    lx = (me // 2 % n_x - core) % n_x
    ly = (me // (2 * n_x) - core) % n_y
    x_bits = n_x.bit_length() - 1
    y_bits = n_y.bit_length() - 1
    held = held.reshape((2,) * y_bits + (2,) * x_bits + (width,))
    names = ["y%d" % b for b in reversed(range(y_bits))] + ["x%d" % b for b in reversed(range(x_bits))]
    order = []
    for b in range(max(x_bits, y_bits)):
        if b < x_bits:
            order.append(("x", b))
        if b < y_bits:
            order.append(("y", b))
    for step, (kind, b) in enumerate(order):
        pos = names.index("%s%d" % (kind, b))
        coord = lx if kind == "x" else ly
        mine_bit = (coord >> b) & 1
        mine = lax.dynamic_index_in_dim(held, mine_bit, pos, keepdims=False)
        other = lax.dynamic_index_in_dim(held, 1 - mine_bit, pos, keepdims=False)
        pairs = logical_pairs(n_y, n_x, kind == "x", 1 << b)
        if step < 2:
            got = lax.ppermute(other.astype(bf16), "dom", pairs).astype(f32)
        else:
            got = lax.ppermute(other, "dom", pairs)
        held = mine + got
        names.pop(pos)
    share = held.reshape(-1)
    n_region = lax.axis_size("region")
    step = 1
    while step < n_region:
        share = share + swapped(share, "region", step)
        step *= 2
    pieces = []
    start = 0
    for t in terms:
        size = t.size // n_dom
        pieces.append(share[start : start + size].reshape(t.shape[0] // n_dom, t.shape[1]))
        start += size
    return pieces


def shards(
    n_x,
    gauges,
    couplings,
    adjacency,
    send_list,
    coverage,
    positive,
    patches,
    message_weight,
    self_weight,
    output_weight,
    patch_weight,
):
    f32 = jnp.float32
    bf16 = jnp.bfloat16
    width = gauges.shape[1]
    wide = patches.shape[1]
    count = couplings.shape[0]
    blocks = gauges.reshape(count, BLOCK, width)
    patch_blocks = patches.reshape(-1, BLOCK, wide)
    block_table, patch_table = neighbour_tables(blocks, send_list, patch_blocks)
    picked = block_table[adjacency]
    message = (
        jnp.einsum("bkij,bkjd->bid", couplings, picked, preferred_element_type=f32)
        .astype(bf16)
        .reshape(-1, width)
    )
    pre_act = jnp.dot(message, message_weight, preferred_element_type=f32) + jnp.dot(
        gauges, self_weight, preferred_element_type=f32
    )
    hidden = (gauges.astype(f32) + jax.nn.silu(pre_act)).astype(bf16)
    queries = jnp.dot(hidden, output_weight, preferred_element_type=f32).astype(bf16)
    table_keys = (
        jnp.dot(patch_table.reshape(-1, wide), patch_weight, preferred_element_type=f32)
        .astype(bf16)
        .reshape(patch_table.shape)
    )
    key_rows = table_keys[coverage].reshape(count, -1, wide)
    flat_cover = patch_table[coverage].reshape(-1, wide)
    query_blocks = queries.reshape(count, BLOCK, wide)
    inv_root = 1.0 / math.sqrt(wide)
    logits = (
        jnp.einsum("bie,bje->bij", query_blocks, key_rows, preferred_element_type=f32) * inv_root
    )
    soft = jax.nn.softmax(logits, axis=-1)
    columns = jnp.arange(logits.shape[2], dtype=jnp.int32)
    target = (positive.reshape(count, BLOCK)[:, :, None] == columns).astype(f32)
    total_gauges = gauges.shape[0] * lax.axis_size("region") * lax.axis_size("dom")
    loss_scale = loss_gain / math.sqrt(total_gauges)
    logit_grad = lax.optimization_barrier(((soft - target) * loss_scale).astype(bf16))
    query_grad = (
        (jnp.einsum("bij,bje->bie", logit_grad, key_rows, preferred_element_type=f32) * inv_root)
        .astype(bf16)
        .reshape(-1, wide)
    )
    key_grad = (
        (
            jnp.einsum("bij,bie->bje", logit_grad, query_blocks, preferred_element_type=f32)
            * inv_root
        )
        .astype(bf16)
        .reshape(-1, wide)
    )
    grad_patch = jnp.dot(flat_cover.T, key_grad, preferred_element_type=f32)
    grad_output = jnp.dot(hidden.T, query_grad, preferred_element_type=f32)
    hidden_grad = jnp.dot(query_grad, output_weight.T, preferred_element_type=f32)
    act_grad = (hidden_grad * silu_slope(pre_act)).astype(bf16)
    grad_message = jnp.dot(message.T, act_grad, preferred_element_type=f32)
    grad_self = jnp.dot(gauges.T, act_grad, preferred_element_type=f32)
    shares = reduce_to_share(
        [grad_message, grad_self, grad_output, grad_patch], lax.axis_size("dom"), n_x
    )
    return tuple(s.astype(bf16) for s in shares)


def solution(mesh):
    placed = (
        P(("region", "dom"), None),
        P(("region", "dom"), None, None, None),
        P(("region", "dom"), None),
        P(("region", "dom")),
        P(("region", "dom"), None),
        P(("region", "dom")),
        P(("region", "dom"), None),
        P(),
        P(),
        P(),
        P(),
    )
    n_x = len({device.coords[0] for device in mesh.devices.flat})
    return jax.shard_map(
        functools.partial(shards, n_x),
        mesh=mesh,
        in_specs=placed,
        out_specs=(P("dom", None), P("dom", None), P("dom", None), P("dom", None)),
        check_vma=False,
    )
```

```python
import functools
import math

import jax
import jax.numpy as jnp
from jax import lax
from jax.sharding import PartitionSpec as P

BLOCK = 128


loss_gain = 16.0
offsets_by = (1, 2, -1, -2)


def passed_along(shard, axis, by):
    count = lax.axis_size(axis)
    return lax.ppermute(shard, axis, [(i, (i + by) % count) for i in range(count)])


def swapped(shard, axis, mask):
    count = lax.axis_size(axis)
    return lax.ppermute(shard, axis, [(i, i ^ mask) for i in range(count)])


def silu_slope(argument):
    sigmoid_v = jax.nn.sigmoid(argument)
    return sigmoid_v * (1.0 + argument * (1.0 - sigmoid_v))


def neighbour_tables(blocks, send_list, patch_blocks):
    outgoing = blocks[send_list]
    n_send = outgoing.shape[0]
    gauge_size = outgoing.size
    packed = jnp.concatenate([outgoing.reshape(-1), patch_blocks.reshape(-1)])
    block_parts = [blocks]
    patch_parts = [patch_blocks]
    for step_by in offsets_by:
        got = passed_along(packed, "dom", step_by)
        block_parts.append(got[:gauge_size].reshape(n_send, BLOCK, blocks.shape[2]))
        patch_parts.append(got[gauge_size:].reshape(patch_blocks.shape))
    return jnp.concatenate(block_parts, axis=0), jnp.concatenate(patch_parts, axis=0)


def logical_pairs(n_y, n_x, axis_is_x, mask):
    pairs = []
    for y in range(n_y):
        for x in range(n_x):
            for c in range(2):
                lx, ly = (x - c) % n_x, (y - c) % n_y
                if axis_is_x:
                    lx ^= mask
                else:
                    ly ^= mask
                px, py = (lx + c) % n_x, (ly + c) % n_y
                pairs.append(((y * n_x + x) * 2 + c, (py * n_x + px) * 2 + c))
    return pairs


def share_order(rows, n_dom, n_x):
    n_y = n_dom // (2 * n_x)
    per = rows // n_dom
    order = []
    for c in range(2):
        for ly in range(n_y):
            for lx in range(n_x):
                d = ((ly + c) % n_y * n_x + (lx + c) % n_x) * 2 + c
                order.extend(range(d * per, (d + 1) * per))
    return jnp.array(order, dtype=jnp.int32)


def reduce_to_share(terms, n_dom, n_x):
    bf16 = jnp.bfloat16
    f32 = jnp.float32
    n_y = n_dom // (2 * n_x)
    flat = jnp.concatenate(
        [t[share_order(t.shape[0], n_dom, n_x)].reshape(2, n_y * n_x, -1) for t in terms], axis=2
    )
    width = flat.shape[2]
    me = lax.axis_index("dom")
    core = me % 2
    mine = lax.dynamic_index_in_dim(flat, core, 0, keepdims=False)
    other = lax.dynamic_index_in_dim(flat, 1 - core, 0, keepdims=False)
    held = mine + swapped(other, "dom", 1)
    lx = (me // 2 % n_x - core) % n_x
    ly = (me // (2 * n_x) - core) % n_y
    x_bits = n_x.bit_length() - 1
    y_bits = n_y.bit_length() - 1
    held = held.reshape((2,) * y_bits + (2,) * x_bits + (width,))
    names = ["y%d" % b for b in reversed(range(y_bits))] + ["x%d" % b for b in reversed(range(x_bits))]
    order = []
    for b in range(max(x_bits, y_bits)):
        if b < x_bits:
            order.append(("x", b))
        if b < y_bits:
            order.append(("y", b))
    for step, (kind, b) in enumerate(order):
        pos = names.index("%s%d" % (kind, b))
        coord = lx if kind == "x" else ly
        mine_bit = (coord >> b) & 1
        mine = lax.dynamic_index_in_dim(held, mine_bit, pos, keepdims=False)
        other = lax.dynamic_index_in_dim(held, 1 - mine_bit, pos, keepdims=False)
        pairs = logical_pairs(n_y, n_x, kind == "x", 1 << b)
        if step < 2:
            got = lax.ppermute(other.astype(bf16), "dom", pairs).astype(f32)
        else:
            got = lax.ppermute(other, "dom", pairs)
        held = mine + got
        names.pop(pos)
    share = held.reshape(-1)
    n_region = lax.axis_size("region")
    step = 1
    while step < n_region:
        share = share + swapped(share, "region", step)
        step *= 2
    pieces = []
    start = 0
    for t in terms:
        size = t.size // n_dom
        pieces.append(share[start : start + size].reshape(t.shape[0] // n_dom, t.shape[1]))
        start += size
    return pieces


def shards(
    n_x,
    gauges,
    couplings,
    adjacency,
    send_list,
    coverage,
    positive,
    patches,
    message_weight,
    self_weight,
    output_weight,
    patch_weight,
):
    f32 = jnp.float32
    bf16 = jnp.bfloat16
    width = gauges.shape[1]
    wide = patches.shape[1]
    count = couplings.shape[0]
    blocks = gauges.reshape(count, BLOCK, width)
    patch_blocks = patches.reshape(-1, BLOCK, wide)
    block_table, patch_table = neighbour_tables(blocks, send_list, patch_blocks)
    picked = block_table[adjacency]
    message = (
        jnp.einsum("bkij,bkjd->bid", couplings, picked, preferred_element_type=f32)
        .astype(bf16)
        .reshape(-1, width)
    )
    pre_act = jnp.dot(message, message_weight, preferred_element_type=f32) + jnp.dot(
        gauges, self_weight, preferred_element_type=f32
    )
    hidden = (gauges.astype(f32) + jax.nn.silu(pre_act)).astype(bf16)
    queries = jnp.dot(hidden, output_weight, preferred_element_type=f32).astype(bf16)
    table_keys = (
        jnp.dot(patch_table.reshape(-1, wide), patch_weight, preferred_element_type=f32)
        .astype(bf16)
        .reshape(patch_table.shape)
    )
    key_rows = table_keys[coverage].reshape(count, -1, wide)
    flat_cover = patch_table[coverage].reshape(-1, wide)
    query_blocks = queries.reshape(count, BLOCK, wide)
    inv_root = 1.0 / math.sqrt(wide)
    logits = (
        jnp.einsum("bie,bje->bij", query_blocks, key_rows, preferred_element_type=f32) * inv_root
    )
    soft = jax.nn.softmax(logits, axis=-1)
    columns = jnp.arange(logits.shape[2], dtype=jnp.int32)
    target = (positive.reshape(count, BLOCK)[:, :, None] == columns).astype(f32)
    total_gauges = gauges.shape[0] * lax.axis_size("region") * lax.axis_size("dom")
    loss_scale = loss_gain / math.sqrt(total_gauges)
    logit_grad = lax.optimization_barrier(((soft - target) * loss_scale).astype(bf16))
    query_grad = (
        (jnp.einsum("bij,bje->bie", logit_grad, key_rows, preferred_element_type=f32) * inv_root)
        .astype(bf16)
        .reshape(-1, wide)
    )
    key_grad = (
        (
            jnp.einsum("bij,bie->bje", logit_grad, query_blocks, preferred_element_type=f32)
            * inv_root
        )
        .astype(bf16)
        .reshape(-1, wide)
    )
    grad_patch = jnp.dot(flat_cover.T, key_grad, preferred_element_type=f32)
    grad_output = jnp.dot(hidden.T, query_grad, preferred_element_type=f32)
    hidden_grad = jnp.dot(query_grad, output_weight.T, preferred_element_type=f32)
    act_grad = (hidden_grad * silu_slope(pre_act)).astype(bf16)
    grad_message = jnp.dot(message.T, act_grad, preferred_element_type=f32)
    grad_self = jnp.dot(gauges.T, act_grad, preferred_element_type=f32)
    shares = reduce_to_share(
        [grad_message, grad_self, grad_output, grad_patch], lax.axis_size("dom"), n_x
    )
    return tuple(s.astype(bf16) for s in shares)


def solution(mesh):
    placed = (
        P(("region", "dom"), None),
        P(("region", "dom"), None, None, None),
        P(("region", "dom"), None),
        P(("region", "dom")),
        P(("region", "dom"), None),
        P(("region", "dom")),
        P(("region", "dom"), None),
        P(),
        P(),
        P(),
        P(),
    )
    n_x = len({device.coords[0] for device in mesh.devices.flat})
    return jax.shard_map(
        functools.partial(shards, n_x),
        mesh=mesh,
        in_specs=placed,
        out_specs=(P("dom", None), P("dom", None), P("dom", None), P("dom", None)),
        check_vma=False,
    )
```

```python
import functools
import math

import jax
import jax.numpy as jnp
from jax import lax
from jax.sharding import PartitionSpec as P

BLOCK = 128


loss_gain = 16.0
offsets_by = (1, 2, -1, -2)


def passed_along(shard, axis, by):
    count = lax.axis_size(axis)
    return lax.ppermute(shard, axis, [(i, (i + by) % count) for i in range(count)])


def swapped(shard, axis, mask):
    count = lax.axis_size(axis)
    return lax.ppermute(shard, axis, [(i, i ^ mask) for i in range(count)])


def silu_slope(argument):
    sigmoid_v = jax.nn.sigmoid(argument)
    return sigmoid_v * (1.0 + argument * (1.0 - sigmoid_v))


def neighbour_tables(blocks, send_list, patch_blocks):
    outgoing = blocks[send_list]
    n_send = outgoing.shape[0]
    gauge_size = outgoing.size
    packed = jnp.concatenate([outgoing.reshape(-1), patch_blocks.reshape(-1)])
    block_parts = [blocks]
    patch_parts = [patch_blocks]
    for step_by in offsets_by:
        got = passed_along(packed, "dom", step_by)
        block_parts.append(got[:gauge_size].reshape(n_send, BLOCK, blocks.shape[2]))
        patch_parts.append(got[gauge_size:].reshape(patch_blocks.shape))
    return jnp.concatenate(block_parts, axis=0), jnp.concatenate(patch_parts, axis=0)


def logical_pairs(n_y, n_x, axis_is_x, mask):
    pairs = []
    for y in range(n_y):
        for x in range(n_x):
            for c in range(2):
                lx, ly = (x - c) % n_x, (y - c) % n_y
                if axis_is_x:
                    lx ^= mask
                else:
                    ly ^= mask
                px, py = (lx + c) % n_x, (ly + c) % n_y
                pairs.append(((y * n_x + x) * 2 + c, (py * n_x + px) * 2 + c))
    return pairs


def halving_steps(n_y, n_x):
    x_bits = n_x.bit_length() - 1
    y_bits = n_y.bit_length() - 1
    order = []
    for b in range(max(x_bits, y_bits)):
        if b < x_bits:
            order.append(("x", b))
        if b < y_bits:
            order.append(("y", b))
    return order


def share_order(rows, n_dom, n_x):
    n_y = n_dom // (2 * n_x)
    per = rows // n_dom
    steps = halving_steps(n_y, n_x)
    slots = [None] * n_dom
    for c in range(2):
        for ly in range(n_y):
            for lx in range(n_x):
                d = ((ly + c) % n_y * n_x + (lx + c) % n_x) * 2 + c
                slot = c
                for kind, b in steps:
                    slot = slot * 2 + (((lx if kind == "x" else ly) >> b) & 1)
                slots[slot] = d
    order = []
    for d in slots:
        order.extend(range(d * per, (d + 1) * per))
    return jnp.array(order, dtype=jnp.int32)


def reduce_to_share(terms, n_dom, n_x):
    bf16 = jnp.bfloat16
    f32 = jnp.float32
    n_y = n_dom // (2 * n_x)
    flat = jnp.concatenate(
        [t[share_order(t.shape[0], n_dom, n_x)].reshape(2, n_y * n_x, -1) for t in terms], axis=2
    )
    width = flat.shape[2]
    me = lax.axis_index("dom")
    core = me % 2
    mine = lax.dynamic_index_in_dim(flat, core, 0, keepdims=False)
    other = lax.dynamic_index_in_dim(flat, 1 - core, 0, keepdims=False)
    held = mine + swapped(other, "dom", 1)
    lx = (me // 2 % n_x - core) % n_x
    ly = (me // (2 * n_x) - core) % n_y
    for step, (kind, b) in enumerate(halving_steps(n_y, n_x)):
        held = held.reshape(2, -1, width)
        coord = lx if kind == "x" else ly
        mine_bit = (coord >> b) & 1
        mine = lax.dynamic_index_in_dim(held, mine_bit, 0, keepdims=False)
        other = lax.dynamic_index_in_dim(held, 1 - mine_bit, 0, keepdims=False)
        pairs = logical_pairs(n_y, n_x, kind == "x", 1 << b)
        if step < 2:
            got = lax.ppermute(other.astype(bf16), "dom", pairs).astype(f32)
        else:
            got = lax.ppermute(other, "dom", pairs)
        held = mine + got
    share = held.reshape(-1)
    n_region = lax.axis_size("region")
    step = 1
    while step < n_region:
        share = share + swapped(share, "region", step)
        step *= 2
    pieces = []
    start = 0
    for t in terms:
        size = t.size // n_dom
        pieces.append(share[start : start + size].reshape(t.shape[0] // n_dom, t.shape[1]))
        start += size
    return pieces


def shards(
    n_x,
    gauges,
    couplings,
    adjacency,
    send_list,
    coverage,
    positive,
    patches,
    message_weight,
    self_weight,
    output_weight,
    patch_weight,
):
    f32 = jnp.float32
    bf16 = jnp.bfloat16
    width = gauges.shape[1]
    wide = patches.shape[1]
    count = couplings.shape[0]
    blocks = gauges.reshape(count, BLOCK, width)
    patch_blocks = patches.reshape(-1, BLOCK, wide)
    block_table, patch_table = neighbour_tables(blocks, send_list, patch_blocks)
    picked = block_table[adjacency]
    message = (
        jnp.einsum("bkij,bkjd->bid", couplings, picked, preferred_element_type=f32)
        .astype(bf16)
        .reshape(-1, width)
    )
    pre_act = jnp.dot(message, message_weight, preferred_element_type=f32) + jnp.dot(
        gauges, self_weight, preferred_element_type=f32
    )
    hidden = (gauges.astype(f32) + jax.nn.silu(pre_act)).astype(bf16)
    queries = jnp.dot(hidden, output_weight, preferred_element_type=f32).astype(bf16)
    table_keys = (
        jnp.dot(patch_table.reshape(-1, wide), patch_weight, preferred_element_type=f32)
        .astype(bf16)
        .reshape(patch_table.shape)
    )
    key_rows = table_keys[coverage].reshape(count, -1, wide)
    flat_cover = patch_table[coverage].reshape(-1, wide)
    query_blocks = queries.reshape(count, BLOCK, wide)
    inv_root = 1.0 / math.sqrt(wide)
    logits = (
        jnp.einsum("bie,bje->bij", query_blocks, key_rows, preferred_element_type=f32) * inv_root
    )
    soft = jax.nn.softmax(logits, axis=-1)
    columns = jnp.arange(logits.shape[2], dtype=jnp.int32)
    target = (positive.reshape(count, BLOCK)[:, :, None] == columns).astype(f32)
    total_gauges = gauges.shape[0] * lax.axis_size("region") * lax.axis_size("dom")
    loss_scale = loss_gain / math.sqrt(total_gauges)
    logit_grad = lax.optimization_barrier(((soft - target) * loss_scale).astype(bf16))
    query_grad = (
        (jnp.einsum("bij,bje->bie", logit_grad, key_rows, preferred_element_type=f32) * inv_root)
        .astype(bf16)
        .reshape(-1, wide)
    )
    key_grad = (
        (
            jnp.einsum("bij,bie->bje", logit_grad, query_blocks, preferred_element_type=f32)
            * inv_root
        )
        .astype(bf16)
        .reshape(-1, wide)
    )
    grad_patch = jnp.dot(flat_cover.T, key_grad, preferred_element_type=f32)
    grad_output = jnp.dot(hidden.T, query_grad, preferred_element_type=f32)
    hidden_grad = jnp.dot(query_grad, output_weight.T, preferred_element_type=f32)
    act_grad = (hidden_grad * silu_slope(pre_act)).astype(bf16)
    grad_message = jnp.dot(message.T, act_grad, preferred_element_type=f32)
    grad_self = jnp.dot(gauges.T, act_grad, preferred_element_type=f32)
    shares = reduce_to_share(
        [grad_message, grad_self, grad_output, grad_patch], lax.axis_size("dom"), n_x
    )
    return tuple(s.astype(bf16) for s in shares)


def solution(mesh):
    placed = (
        P(("region", "dom"), None),
        P(("region", "dom"), None, None, None),
        P(("region", "dom"), None),
        P(("region", "dom")),
        P(("region", "dom"), None),
        P(("region", "dom")),
        P(("region", "dom"), None),
        P(),
        P(),
        P(),
        P(),
    )
    n_x = len({device.coords[0] for device in mesh.devices.flat})
    return jax.shard_map(
        functools.partial(shards, n_x),
        mesh=mesh,
        in_specs=placed,
        out_specs=(P("dom", None), P("dom", None), P("dom", None), P("dom", None)),
        check_vma=False,
    )
```

```python
import functools
import math

import jax
import jax.numpy as jnp
from jax import lax
from jax.sharding import PartitionSpec as P

BLOCK = 128


loss_gain = 16.0
offsets_by = (1, 2, -1, -2)


def passed_along(shard, axis, by):
    count = lax.axis_size(axis)
    return lax.ppermute(shard, axis, [(i, (i + by) % count) for i in range(count)])


def swapped(shard, axis, mask):
    count = lax.axis_size(axis)
    return lax.ppermute(shard, axis, [(i, i ^ mask) for i in range(count)])


def silu_slope(argument):
    sigmoid_v = jax.nn.sigmoid(argument)
    return sigmoid_v * (1.0 + argument * (1.0 - sigmoid_v))


def neighbour_tables(blocks, send_list, patch_blocks):
    outgoing = blocks[send_list]
    n_send = outgoing.shape[0]
    gauge_size = outgoing.size
    packed = jnp.concatenate([outgoing.reshape(-1), patch_blocks.reshape(-1)])
    block_parts = [blocks]
    patch_parts = [patch_blocks]
    for step_by in offsets_by:
        got = passed_along(packed, "dom", step_by)
        block_parts.append(got[:gauge_size].reshape(n_send, BLOCK, blocks.shape[2]))
        patch_parts.append(got[gauge_size:].reshape(patch_blocks.shape))
    return jnp.concatenate(block_parts, axis=0), jnp.concatenate(patch_parts, axis=0)


def logical_pairs(n_y, n_x, axis_is_x, mask):
    pairs = []
    for y in range(n_y):
        for x in range(n_x):
            for c in range(2):
                lx, ly = (x - c) % n_x, (y - c) % n_y
                if axis_is_x:
                    lx ^= mask
                else:
                    ly ^= mask
                px, py = (lx + c) % n_x, (ly + c) % n_y
                pairs.append(((y * n_x + x) * 2 + c, (py * n_x + px) * 2 + c))
    return pairs


def halving_steps(n_y, n_x):
    x_bits = n_x.bit_length() - 1
    y_bits = n_y.bit_length() - 1
    order = []
    for b in range(max(x_bits, y_bits)):
        if b < x_bits:
            order.append(("x", b))
        if b < y_bits:
            order.append(("y", b))
    return order


def share_order(rows, n_dom, n_x):
    n_y = n_dom // (2 * n_x)
    per = rows // n_dom
    steps = halving_steps(n_y, n_x)
    slots = [None] * n_dom
    for c in range(2):
        for ly in range(n_y):
            for lx in range(n_x):
                d = ((ly + c) % n_y * n_x + (lx + c) % n_x) * 2 + c
                slot = c
                for kind, b in steps:
                    slot = slot * 2 + (((lx if kind == "x" else ly) >> b) & 1)
                slots[slot] = d
    order = []
    for d in slots:
        order.extend(range(d * per, (d + 1) * per))
    return jnp.array(order, dtype=jnp.int32)


def reduce_to_share(terms, n_dom, n_x):
    bf16 = jnp.bfloat16
    f32 = jnp.float32
    n_y = n_dom // (2 * n_x)
    flat = jnp.concatenate(
        [t[share_order(t.shape[0], n_dom, n_x)].reshape(2, n_y * n_x, -1) for t in terms], axis=2
    )
    width = flat.shape[2]
    me = lax.axis_index("dom")
    core = me % 2
    mine = lax.dynamic_index_in_dim(flat, core, 0, keepdims=False)
    other = lax.dynamic_index_in_dim(flat, 1 - core, 0, keepdims=False)
    held = mine + swapped(other, "dom", 1)
    lx = (me // 2 % n_x - core) % n_x
    ly = (me // (2 * n_x) - core) % n_y
    for step, (kind, b) in enumerate(halving_steps(n_y, n_x)):
        held = held.reshape(2, -1, width)
        coord = lx if kind == "x" else ly
        mine_bit = (coord >> b) & 1
        mine = lax.dynamic_index_in_dim(held, mine_bit, 0, keepdims=False)
        other = lax.dynamic_index_in_dim(held, 1 - mine_bit, 0, keepdims=False)
        pairs = logical_pairs(n_y, n_x, kind == "x", 1 << b)
        if step < 4:
            got = lax.ppermute(other.astype(bf16), "dom", pairs).astype(f32)
        else:
            got = lax.ppermute(other, "dom", pairs)
        held = mine + got
    share = held.reshape(-1)
    n_region = lax.axis_size("region")
    step = 1
    while step < n_region:
        share = share + swapped(share, "region", step)
        step *= 2
    pieces = []
    start = 0
    for t in terms:
        size = t.size // n_dom
        pieces.append(share[start : start + size].reshape(t.shape[0] // n_dom, t.shape[1]))
        start += size
    return pieces


def shards(
    n_x,
    gauges,
    couplings,
    adjacency,
    send_list,
    coverage,
    positive,
    patches,
    message_weight,
    self_weight,
    output_weight,
    patch_weight,
):
    f32 = jnp.float32
    bf16 = jnp.bfloat16
    width = gauges.shape[1]
    wide = patches.shape[1]
    count = couplings.shape[0]
    blocks = gauges.reshape(count, BLOCK, width)
    patch_blocks = patches.reshape(-1, BLOCK, wide)
    block_table, patch_table = neighbour_tables(blocks, send_list, patch_blocks)
    picked = block_table[adjacency]
    message = (
        jnp.einsum("bkij,bkjd->bid", couplings, picked, preferred_element_type=f32)
        .astype(bf16)
        .reshape(-1, width)
    )
    pre_act = jnp.dot(message, message_weight, preferred_element_type=f32) + jnp.dot(
        gauges, self_weight, preferred_element_type=f32
    )
    hidden = (gauges.astype(f32) + jax.nn.silu(pre_act)).astype(bf16)
    queries = jnp.dot(hidden, output_weight, preferred_element_type=f32).astype(bf16)
    table_keys = (
        jnp.dot(patch_table.reshape(-1, wide), patch_weight, preferred_element_type=f32)
        .astype(bf16)
        .reshape(patch_table.shape)
    )
    key_rows = table_keys[coverage].reshape(count, -1, wide)
    flat_cover = patch_table[coverage].reshape(-1, wide)
    query_blocks = queries.reshape(count, BLOCK, wide)
    inv_root = 1.0 / math.sqrt(wide)
    logits = (
        jnp.einsum("bie,bje->bij", query_blocks, key_rows, preferred_element_type=f32) * inv_root
    )
    soft = jax.nn.softmax(logits, axis=-1)
    columns = jnp.arange(logits.shape[2], dtype=jnp.int32)
    target = (positive.reshape(count, BLOCK)[:, :, None] == columns).astype(f32)
    total_gauges = gauges.shape[0] * lax.axis_size("region") * lax.axis_size("dom")
    loss_scale = loss_gain / math.sqrt(total_gauges)
    logit_grad = lax.optimization_barrier(((soft - target) * loss_scale).astype(bf16))
    query_grad = (
        (jnp.einsum("bij,bje->bie", logit_grad, key_rows, preferred_element_type=f32) * inv_root)
        .astype(bf16)
        .reshape(-1, wide)
    )
    key_grad = (
        (
            jnp.einsum("bij,bie->bje", logit_grad, query_blocks, preferred_element_type=f32)
            * inv_root
        )
        .astype(bf16)
        .reshape(-1, wide)
    )
    grad_patch = jnp.dot(flat_cover.T, key_grad, preferred_element_type=f32)
    grad_output = jnp.dot(hidden.T, query_grad, preferred_element_type=f32)
    hidden_grad = jnp.dot(query_grad, output_weight.T, preferred_element_type=f32)
    act_grad = (hidden_grad * silu_slope(pre_act)).astype(bf16)
    grad_message = jnp.dot(message.T, act_grad, preferred_element_type=f32)
    grad_self = jnp.dot(gauges.T, act_grad, preferred_element_type=f32)
    shares = reduce_to_share(
        [grad_message, grad_self, grad_output, grad_patch], lax.axis_size("dom"), n_x
    )
    return tuple(s.astype(bf16) for s in shares)


def solution(mesh):
    placed = (
        P(("region", "dom"), None),
        P(("region", "dom"), None, None, None),
        P(("region", "dom"), None),
        P(("region", "dom")),
        P(("region", "dom"), None),
        P(("region", "dom")),
        P(("region", "dom"), None),
        P(),
        P(),
        P(),
        P(),
    )
    n_x = len({device.coords[0] for device in mesh.devices.flat})
    return jax.shard_map(
        functools.partial(shards, n_x),
        mesh=mesh,
        in_specs=placed,
        out_specs=(P("dom", None), P("dom", None), P("dom", None), P("dom", None)),
        check_vma=False,
    )
```

```python
import functools
import math

import jax
import jax.numpy as jnp
from jax import lax
from jax.sharding import PartitionSpec as P

BLOCK = 128


loss_gain = 16.0
offsets_by = (1, 2, -1, -2)


def passed_along(shard, axis, by):
    count = lax.axis_size(axis)
    return lax.ppermute(shard, axis, [(i, (i + by) % count) for i in range(count)])


def swapped(shard, axis, mask):
    count = lax.axis_size(axis)
    return lax.ppermute(shard, axis, [(i, i ^ mask) for i in range(count)])


def silu_slope(argument):
    sigmoid_v = jax.nn.sigmoid(argument)
    return sigmoid_v * (1.0 + argument * (1.0 - sigmoid_v))


def neighbour_tables(blocks, send_list, patch_blocks):
    outgoing = blocks[send_list]
    n_send = outgoing.shape[0]
    gauge_size = outgoing.size
    packed = jnp.concatenate([outgoing.reshape(-1), patch_blocks.reshape(-1)])
    block_parts = [blocks]
    patch_parts = [patch_blocks]
    for step_by in offsets_by:
        got = passed_along(packed, "dom", step_by)
        block_parts.append(got[:gauge_size].reshape(n_send, BLOCK, blocks.shape[2]))
        patch_parts.append(got[gauge_size:].reshape(patch_blocks.shape))
    return jnp.concatenate(block_parts, axis=0), jnp.concatenate(patch_parts, axis=0)


def logical_pairs(n_y, n_x, axis_is_x, mask):
    pairs = []
    for y in range(n_y):
        for x in range(n_x):
            for c in range(2):
                lx, ly = (x - c) % n_x, (y - c) % n_y
                if axis_is_x:
                    lx ^= mask
                else:
                    ly ^= mask
                px, py = (lx + c) % n_x, (ly + c) % n_y
                pairs.append(((y * n_x + x) * 2 + c, (py * n_x + px) * 2 + c))
    return pairs


def halving_steps(n_y):
    return [("y", b) for b in range(n_y.bit_length() - 1)]


def share_order(rows, n_dom, n_x):
    n_y = n_dom // (2 * n_x)
    per = rows // n_dom
    steps = halving_steps(n_y)
    slots = [None] * n_dom
    for c in range(2):
        for ly in range(n_y):
            for lx in range(n_x):
                d = ((ly + c) % n_y * n_x + (lx + c) % n_x) * 2 + c
                slot = c * n_x + lx
                for _, b in steps:
                    slot = slot * 2 + ((ly >> b) & 1)
                slots[slot] = d
    order = []
    for d in slots:
        order.extend(range(d * per, (d + 1) * per))
    return jnp.array(order, dtype=jnp.int32)


def shifted_x(shard, n_y, n_x, by):
    pairs = []
    for y in range(n_y):
        for x in range(n_x):
            for c in range(2):
                pairs.append(((y * n_x + x) * 2 + c, (y * n_x + (x + by) % n_x) * 2 + c))
    return lax.ppermute(shard, "dom", pairs)


def reduce_to_share(terms, n_dom, n_x):
    bf16 = jnp.bfloat16
    f32 = jnp.float32
    n_y = n_dom // (2 * n_x)
    flat = jnp.concatenate(
        [t[share_order(t.shape[0], n_dom, n_x)].reshape(2, n_y * n_x, -1) for t in terms], axis=2
    )
    width = flat.shape[2]
    me = lax.axis_index("dom")
    core = me % 2
    mine = lax.dynamic_index_in_dim(flat, core, 0, keepdims=False)
    other = lax.dynamic_index_in_dim(flat, 1 - core, 0, keepdims=False)
    held = mine + swapped(other, "dom", 1)
    lx = (me // 2 % n_x - core) % n_x
    ly = (me // (2 * n_x) - core) % n_y
    held = held.reshape(n_x, -1, width)
    total = lax.dynamic_index_in_dim(held, lx, 0, keepdims=False)
    for by in range(1, n_x):
        block = lax.dynamic_index_in_dim(held, (lx + by) % n_x, 0, keepdims=False)
        total = total + shifted_x(block.astype(bf16), n_y, n_x, by).astype(f32)
    held = total
    for step, (kind, b) in enumerate(halving_steps(n_y)):
        held = held.reshape(2, -1, width)
        mine_bit = (ly >> b) & 1
        mine = lax.dynamic_index_in_dim(held, mine_bit, 0, keepdims=False)
        other = lax.dynamic_index_in_dim(held, 1 - mine_bit, 0, keepdims=False)
        pairs = logical_pairs(n_y, n_x, False, 1 << b)
        if step < 2:
            got = lax.ppermute(other.astype(bf16), "dom", pairs).astype(f32)
        else:
            got = lax.ppermute(other, "dom", pairs)
        held = mine + got
    share = held.reshape(-1)
    n_region = lax.axis_size("region")
    step = 1
    while step < n_region:
        share = share + swapped(share, "region", step)
        step *= 2
    pieces = []
    start = 0
    for t in terms:
        size = t.size // n_dom
        pieces.append(share[start : start + size].reshape(t.shape[0] // n_dom, t.shape[1]))
        start += size
    return pieces


def shards(
    n_x,
    gauges,
    couplings,
    adjacency,
    send_list,
    coverage,
    positive,
    patches,
    message_weight,
    self_weight,
    output_weight,
    patch_weight,
):
    f32 = jnp.float32
    bf16 = jnp.bfloat16
    width = gauges.shape[1]
    wide = patches.shape[1]
    count = couplings.shape[0]
    blocks = gauges.reshape(count, BLOCK, width)
    patch_blocks = patches.reshape(-1, BLOCK, wide)
    block_table, patch_table = neighbour_tables(blocks, send_list, patch_blocks)
    picked = block_table[adjacency]
    message = (
        jnp.einsum("bkij,bkjd->bid", couplings, picked, preferred_element_type=f32)
        .astype(bf16)
        .reshape(-1, width)
    )
    pre_act = jnp.dot(message, message_weight, preferred_element_type=f32) + jnp.dot(
        gauges, self_weight, preferred_element_type=f32
    )
    hidden = (gauges.astype(f32) + jax.nn.silu(pre_act)).astype(bf16)
    queries = jnp.dot(hidden, output_weight, preferred_element_type=f32).astype(bf16)
    table_keys = (
        jnp.dot(patch_table.reshape(-1, wide), patch_weight, preferred_element_type=f32)
        .astype(bf16)
        .reshape(patch_table.shape)
    )
    key_rows = table_keys[coverage].reshape(count, -1, wide)
    flat_cover = patch_table[coverage].reshape(-1, wide)
    query_blocks = queries.reshape(count, BLOCK, wide)
    inv_root = 1.0 / math.sqrt(wide)
    logits = (
        jnp.einsum("bie,bje->bij", query_blocks, key_rows, preferred_element_type=f32) * inv_root
    )
    soft = jax.nn.softmax(logits, axis=-1)
    columns = jnp.arange(logits.shape[2], dtype=jnp.int32)
    target = (positive.reshape(count, BLOCK)[:, :, None] == columns).astype(f32)
    total_gauges = gauges.shape[0] * lax.axis_size("region") * lax.axis_size("dom")
    loss_scale = loss_gain / math.sqrt(total_gauges)
    logit_grad = lax.optimization_barrier(((soft - target) * loss_scale).astype(bf16))
    query_grad = (
        (jnp.einsum("bij,bje->bie", logit_grad, key_rows, preferred_element_type=f32) * inv_root)
        .astype(bf16)
        .reshape(-1, wide)
    )
    key_grad = (
        (
            jnp.einsum("bij,bie->bje", logit_grad, query_blocks, preferred_element_type=f32)
            * inv_root
        )
        .astype(bf16)
        .reshape(-1, wide)
    )
    grad_patch = jnp.dot(flat_cover.T, key_grad, preferred_element_type=f32)
    grad_output = jnp.dot(hidden.T, query_grad, preferred_element_type=f32)
    hidden_grad = jnp.dot(query_grad, output_weight.T, preferred_element_type=f32)
    act_grad = (hidden_grad * silu_slope(pre_act)).astype(bf16)
    grad_message = jnp.dot(message.T, act_grad, preferred_element_type=f32)
    grad_self = jnp.dot(gauges.T, act_grad, preferred_element_type=f32)
    shares = reduce_to_share(
        [grad_message, grad_self, grad_output, grad_patch], lax.axis_size("dom"), n_x
    )
    return tuple(s.astype(bf16) for s in shares)


def solution(mesh):
    placed = (
        P(("region", "dom"), None),
        P(("region", "dom"), None, None, None),
        P(("region", "dom"), None),
        P(("region", "dom")),
        P(("region", "dom"), None),
        P(("region", "dom")),
        P(("region", "dom"), None),
        P(),
        P(),
        P(),
        P(),
    )
    n_x = len({device.coords[0] for device in mesh.devices.flat})
    return jax.shard_map(
        functools.partial(shards, n_x),
        mesh=mesh,
        in_specs=placed,
        out_specs=(P("dom", None), P("dom", None), P("dom", None), P("dom", None)),
        check_vma=False,
    )
```

```python
import functools
import math

import jax
import jax.numpy as jnp
from jax import lax
from jax.sharding import PartitionSpec as P

BLOCK = 128


loss_gain = 16.0
offsets_by = (1, 2, -1, -2)


def passed_along(shard, axis, by):
    count = lax.axis_size(axis)
    return lax.ppermute(shard, axis, [(i, (i + by) % count) for i in range(count)])


def swapped(shard, axis, mask):
    count = lax.axis_size(axis)
    return lax.ppermute(shard, axis, [(i, i ^ mask) for i in range(count)])


def silu_slope(argument):
    sigmoid_v = jax.nn.sigmoid(argument)
    return sigmoid_v * (1.0 + argument * (1.0 - sigmoid_v))


def neighbour_tables(blocks, send_list, patch_blocks):
    outgoing = blocks[send_list]
    n_send = outgoing.shape[0]
    gauge_size = outgoing.size
    packed = jnp.concatenate([outgoing.reshape(-1), patch_blocks.reshape(-1)])
    block_parts = [blocks]
    patch_parts = [patch_blocks]
    for step_by in offsets_by:
        got = passed_along(packed, "dom", step_by)
        block_parts.append(got[:gauge_size].reshape(n_send, BLOCK, blocks.shape[2]))
        patch_parts.append(got[gauge_size:].reshape(patch_blocks.shape))
    return jnp.concatenate(block_parts, axis=0), jnp.concatenate(patch_parts, axis=0)


def logical_pairs(n_y, n_x, axis_is_x, mask):
    pairs = []
    for y in range(n_y):
        for x in range(n_x):
            for c in range(2):
                lx, ly = (x - c) % n_x, (y - c) % n_y
                if axis_is_x:
                    lx ^= mask
                else:
                    ly ^= mask
                px, py = (lx + c) % n_x, (ly + c) % n_y
                pairs.append(((y * n_x + x) * 2 + c, (py * n_x + px) * 2 + c))
    return pairs


def halving_steps(n_y):
    return [("y", b) for b in range(n_y.bit_length() - 1)]


def share_order(rows, n_dom, n_x):
    n_y = n_dom // (2 * n_x)
    per = rows // n_dom
    steps = halving_steps(n_y)
    slots = [None] * n_dom
    for c in range(2):
        for ly in range(n_y):
            for lx in range(n_x):
                d = ((ly + c) % n_y * n_x + (lx + c) % n_x) * 2 + c
                slot = c * n_x + lx
                for _, b in steps:
                    slot = slot * 2 + ((ly >> b) & 1)
                slots[slot] = d
    order = []
    for d in slots:
        order.extend(range(d * per, (d + 1) * per))
    return jnp.array(order, dtype=jnp.int32)


def shifted_x(shard, n_y, n_x, by):
    pairs = []
    for y in range(n_y):
        for x in range(n_x):
            for c in range(2):
                pairs.append(((y * n_x + x) * 2 + c, (y * n_x + (x + by) % n_x) * 2 + c))
    return lax.ppermute(shard, "dom", pairs)


def reduce_to_share(terms, n_dom, n_x):
    bf16 = jnp.bfloat16
    f32 = jnp.float32
    n_y = n_dom // (2 * n_x)
    flat = jnp.concatenate(
        [t[share_order(t.shape[0], n_dom, n_x)].reshape(2, n_y * n_x, -1) for t in terms], axis=2
    )
    width = flat.shape[2]
    me = lax.axis_index("dom")
    core = me % 2
    mine = lax.dynamic_index_in_dim(flat, core, 0, keepdims=False)
    other = lax.dynamic_index_in_dim(flat, 1 - core, 0, keepdims=False)
    held = mine + swapped(other, "dom", 1)
    lx = (me // 2 % n_x - core) % n_x
    ly = (me // (2 * n_x) - core) % n_y
    held = held.reshape(n_x, -1, width)
    total = lax.dynamic_index_in_dim(held, lx, 0, keepdims=False)
    for by in range(1, n_x):
        block = lax.dynamic_index_in_dim(held, (lx + by) % n_x, 0, keepdims=False)
        total = total + shifted_x(block.astype(bf16), n_y, n_x, by).astype(f32)
    held = total
    for step, (kind, b) in enumerate(halving_steps(n_y)):
        held = held.reshape(2, -1, width)
        mine_bit = (ly >> b) & 1
        mine = lax.dynamic_index_in_dim(held, mine_bit, 0, keepdims=False)
        other = lax.dynamic_index_in_dim(held, 1 - mine_bit, 0, keepdims=False)
        pairs = logical_pairs(n_y, n_x, False, 1 << b)
        if step < 2:
            got = lax.ppermute(other.astype(bf16), "dom", pairs).astype(f32)
        else:
            got = lax.ppermute(other, "dom", pairs)
        held = mine + got
    share = held.reshape(-1)
    n_region = lax.axis_size("region")
    region = lax.axis_index("region")
    share = share + swapped(share, "region", 1)
    n_group = n_region // 2
    got = [share] + [passed_along(share, "region", 2 * k) for k in range(1, n_group)]
    ordered = jnp.take(jnp.stack(got), (region // 2 - jnp.arange(n_group)) % n_group, axis=0)
    share = jnp.sum(ordered, axis=0)
    pieces = []
    start = 0
    for t in terms:
        size = t.size // n_dom
        pieces.append(share[start : start + size].reshape(t.shape[0] // n_dom, t.shape[1]))
        start += size
    return pieces


def shards(
    n_x,
    gauges,
    couplings,
    adjacency,
    send_list,
    coverage,
    positive,
    patches,
    message_weight,
    self_weight,
    output_weight,
    patch_weight,
):
    f32 = jnp.float32
    bf16 = jnp.bfloat16
    width = gauges.shape[1]
    wide = patches.shape[1]
    count = couplings.shape[0]
    blocks = gauges.reshape(count, BLOCK, width)
    patch_blocks = patches.reshape(-1, BLOCK, wide)
    block_table, patch_table = neighbour_tables(blocks, send_list, patch_blocks)
    picked = block_table[adjacency]
    message = (
        jnp.einsum("bkij,bkjd->bid", couplings, picked, preferred_element_type=f32)
        .astype(bf16)
        .reshape(-1, width)
    )
    pre_act = jnp.dot(message, message_weight, preferred_element_type=f32) + jnp.dot(
        gauges, self_weight, preferred_element_type=f32
    )
    hidden = (gauges.astype(f32) + jax.nn.silu(pre_act)).astype(bf16)
    queries = jnp.dot(hidden, output_weight, preferred_element_type=f32).astype(bf16)
    table_keys = (
        jnp.dot(patch_table.reshape(-1, wide), patch_weight, preferred_element_type=f32)
        .astype(bf16)
        .reshape(patch_table.shape)
    )
    key_rows = table_keys[coverage].reshape(count, -1, wide)
    flat_cover = patch_table[coverage].reshape(-1, wide)
    query_blocks = queries.reshape(count, BLOCK, wide)
    inv_root = 1.0 / math.sqrt(wide)
    logits = (
        jnp.einsum("bie,bje->bij", query_blocks, key_rows, preferred_element_type=f32) * inv_root
    )
    soft = jax.nn.softmax(logits, axis=-1)
    columns = jnp.arange(logits.shape[2], dtype=jnp.int32)
    target = (positive.reshape(count, BLOCK)[:, :, None] == columns).astype(f32)
    total_gauges = gauges.shape[0] * lax.axis_size("region") * lax.axis_size("dom")
    loss_scale = loss_gain / math.sqrt(total_gauges)
    logit_grad = lax.optimization_barrier(((soft - target) * loss_scale).astype(bf16))
    query_grad = (
        (jnp.einsum("bij,bje->bie", logit_grad, key_rows, preferred_element_type=f32) * inv_root)
        .astype(bf16)
        .reshape(-1, wide)
    )
    key_grad = (
        (
            jnp.einsum("bij,bie->bje", logit_grad, query_blocks, preferred_element_type=f32)
            * inv_root
        )
        .astype(bf16)
        .reshape(-1, wide)
    )
    grad_patch = jnp.dot(flat_cover.T, key_grad, preferred_element_type=f32)
    grad_output = jnp.dot(hidden.T, query_grad, preferred_element_type=f32)
    hidden_grad = jnp.dot(query_grad, output_weight.T, preferred_element_type=f32)
    act_grad = (hidden_grad * silu_slope(pre_act)).astype(bf16)
    grad_message = jnp.dot(message.T, act_grad, preferred_element_type=f32)
    grad_self = jnp.dot(gauges.T, act_grad, preferred_element_type=f32)
    shares = reduce_to_share(
        [grad_message, grad_self, grad_output, grad_patch], lax.axis_size("dom"), n_x
    )
    return tuple(s.astype(bf16) for s in shares)


def solution(mesh):
    placed = (
        P(("region", "dom"), None),
        P(("region", "dom"), None, None, None),
        P(("region", "dom"), None),
        P(("region", "dom")),
        P(("region", "dom"), None),
        P(("region", "dom")),
        P(("region", "dom"), None),
        P(),
        P(),
        P(),
        P(),
    )
    n_x = len({device.coords[0] for device in mesh.devices.flat})
    return jax.shard_map(
        functools.partial(shards, n_x),
        mesh=mesh,
        in_specs=placed,
        out_specs=(P("dom", None), P("dom", None), P("dom", None), P("dom", None)),
        check_vma=False,
    )
```

```python
import functools
import math

import jax
import jax.numpy as jnp
from jax import lax
from jax.sharding import PartitionSpec as P

BLOCK = 128


loss_gain = 16.0
offsets_by = (1, 2, -1, -2)


def passed_along(shard, axis, by):
    count = lax.axis_size(axis)
    return lax.ppermute(shard, axis, [(i, (i + by) % count) for i in range(count)])


def swapped(shard, axis, mask):
    count = lax.axis_size(axis)
    return lax.ppermute(shard, axis, [(i, i ^ mask) for i in range(count)])


def silu_slope(argument):
    sigmoid_v = jax.nn.sigmoid(argument)
    return sigmoid_v * (1.0 + argument * (1.0 - sigmoid_v))


def neighbour_tables(blocks, send_list, patch_blocks):
    outgoing = blocks[send_list]
    n_send = outgoing.shape[0]
    gauge_size = outgoing.size
    packed = jnp.concatenate([outgoing.reshape(-1), patch_blocks.reshape(-1)])
    block_parts = [blocks]
    patch_parts = [patch_blocks]
    for step_by in offsets_by:
        got = passed_along(packed, "dom", step_by)
        block_parts.append(got[:gauge_size].reshape(n_send, BLOCK, blocks.shape[2]))
        patch_parts.append(got[gauge_size:].reshape(patch_blocks.shape))
    return jnp.concatenate(block_parts, axis=0), jnp.concatenate(patch_parts, axis=0)


def logical_pairs(n_y, n_x, axis_is_x, mask):
    pairs = []
    for y in range(n_y):
        for x in range(n_x):
            for c in range(2):
                lx, ly = (x - c) % n_x, (y - c) % n_y
                if axis_is_x:
                    lx ^= mask
                else:
                    ly ^= mask
                px, py = (lx + c) % n_x, (ly + c) % n_y
                pairs.append(((y * n_x + x) * 2 + c, (py * n_x + px) * 2 + c))
    return pairs


def halving_steps(n_y):
    return [("y", b) for b in range(n_y.bit_length() - 1)]


def share_order(rows, n_dom, n_x):
    n_y = n_dom // (2 * n_x)
    per = rows // n_dom
    steps = halving_steps(n_y)
    slots = [None] * n_dom
    for c in range(2):
        for ly in range(n_y):
            for lx in range(n_x):
                d = ((ly + c) % n_y * n_x + (lx + c) % n_x) * 2 + c
                slot = c * n_x + lx
                for _, b in steps:
                    slot = slot * 2 + ((ly >> b) & 1)
                slots[slot] = d
    order = []
    for d in slots:
        order.extend(range(d * per, (d + 1) * per))
    return jnp.array(order, dtype=jnp.int32)


def shifted_x(shard, n_y, n_x, by):
    pairs = []
    for y in range(n_y):
        for x in range(n_x):
            for c in range(2):
                pairs.append(((y * n_x + x) * 2 + c, (y * n_x + (x + by) % n_x) * 2 + c))
    return lax.ppermute(shard, "dom", pairs)


def reduce_to_share(terms, n_dom, n_x):
    bf16 = jnp.bfloat16
    f32 = jnp.float32
    n_y = n_dom // (2 * n_x)
    flat = jnp.concatenate(
        [t[share_order(t.shape[0], n_dom, n_x)].reshape(2, n_y * n_x, -1) for t in terms], axis=2
    )
    width = flat.shape[2]
    me = lax.axis_index("dom")
    core = me % 2
    mine = lax.dynamic_index_in_dim(flat, core, 0, keepdims=False)
    other = lax.dynamic_index_in_dim(flat, 1 - core, 0, keepdims=False)
    held = mine + swapped(other.astype(bf16), "dom", 1).astype(f32)
    lx = (me // 2 % n_x - core) % n_x
    ly = (me // (2 * n_x) - core) % n_y
    held = held.reshape(n_x, -1, width)
    total = lax.dynamic_index_in_dim(held, lx, 0, keepdims=False)
    for by in range(1, n_x):
        block = lax.dynamic_index_in_dim(held, (lx + by) % n_x, 0, keepdims=False)
        total = total + shifted_x(block.astype(bf16), n_y, n_x, by).astype(f32)
    held = total
    for step, (kind, b) in enumerate(halving_steps(n_y)):
        held = held.reshape(2, -1, width)
        mine_bit = (ly >> b) & 1
        mine = lax.dynamic_index_in_dim(held, mine_bit, 0, keepdims=False)
        other = lax.dynamic_index_in_dim(held, 1 - mine_bit, 0, keepdims=False)
        pairs = logical_pairs(n_y, n_x, False, 1 << b)
        if step < 2:
            got = lax.ppermute(other.astype(bf16), "dom", pairs).astype(f32)
        else:
            got = lax.ppermute(other, "dom", pairs)
        held = mine + got
    share = held.reshape(-1)
    n_region = lax.axis_size("region")
    step = 1
    while step < n_region:
        share = share + swapped(share, "region", step)
        step *= 2
    pieces = []
    start = 0
    for t in terms:
        size = t.size // n_dom
        pieces.append(share[start : start + size].reshape(t.shape[0] // n_dom, t.shape[1]))
        start += size
    return pieces


def shards(
    n_x,
    gauges,
    couplings,
    adjacency,
    send_list,
    coverage,
    positive,
    patches,
    message_weight,
    self_weight,
    output_weight,
    patch_weight,
):
    f32 = jnp.float32
    bf16 = jnp.bfloat16
    width = gauges.shape[1]
    wide = patches.shape[1]
    count = couplings.shape[0]
    blocks = gauges.reshape(count, BLOCK, width)
    patch_blocks = patches.reshape(-1, BLOCK, wide)
    block_table, patch_table = neighbour_tables(blocks, send_list, patch_blocks)
    picked = block_table[adjacency]
    message = (
        jnp.einsum("bkij,bkjd->bid", couplings, picked, preferred_element_type=f32)
        .astype(bf16)
        .reshape(-1, width)
    )
    pre_act = jnp.dot(message, message_weight, preferred_element_type=f32) + jnp.dot(
        gauges, self_weight, preferred_element_type=f32
    )
    hidden = (gauges.astype(f32) + jax.nn.silu(pre_act)).astype(bf16)
    queries = jnp.dot(hidden, output_weight, preferred_element_type=f32).astype(bf16)
    table_keys = (
        jnp.dot(patch_table.reshape(-1, wide), patch_weight, preferred_element_type=f32)
        .astype(bf16)
        .reshape(patch_table.shape)
    )
    key_rows = table_keys[coverage].reshape(count, -1, wide)
    flat_cover = patch_table[coverage].reshape(-1, wide)
    query_blocks = queries.reshape(count, BLOCK, wide)
    inv_root = 1.0 / math.sqrt(wide)
    logits = (
        jnp.einsum("bie,bje->bij", query_blocks, key_rows, preferred_element_type=f32) * inv_root
    )
    soft = jax.nn.softmax(logits, axis=-1)
    columns = jnp.arange(logits.shape[2], dtype=jnp.int32)
    target = (positive.reshape(count, BLOCK)[:, :, None] == columns).astype(f32)
    total_gauges = gauges.shape[0] * lax.axis_size("region") * lax.axis_size("dom")
    loss_scale = loss_gain / math.sqrt(total_gauges)
    logit_grad = lax.optimization_barrier(((soft - target) * loss_scale).astype(bf16))
    query_grad = (
        (jnp.einsum("bij,bje->bie", logit_grad, key_rows, preferred_element_type=f32) * inv_root)
        .astype(bf16)
        .reshape(-1, wide)
    )
    key_grad = (
        (
            jnp.einsum("bij,bie->bje", logit_grad, query_blocks, preferred_element_type=f32)
            * inv_root
        )
        .astype(bf16)
        .reshape(-1, wide)
    )
    grad_patch = jnp.dot(flat_cover.T, key_grad, preferred_element_type=f32)
    grad_output = jnp.dot(hidden.T, query_grad, preferred_element_type=f32)
    hidden_grad = jnp.dot(query_grad, output_weight.T, preferred_element_type=f32)
    act_grad = (hidden_grad * silu_slope(pre_act)).astype(bf16)
    grad_message = jnp.dot(message.T, act_grad, preferred_element_type=f32)
    grad_self = jnp.dot(gauges.T, act_grad, preferred_element_type=f32)
    shares = reduce_to_share(
        [grad_message, grad_self, grad_output, grad_patch], lax.axis_size("dom"), n_x
    )
    return tuple(s.astype(bf16) for s in shares)


def solution(mesh):
    placed = (
        P(("region", "dom"), None),
        P(("region", "dom"), None, None, None),
        P(("region", "dom"), None),
        P(("region", "dom")),
        P(("region", "dom"), None),
        P(("region", "dom")),
        P(("region", "dom"), None),
        P(),
        P(),
        P(),
        P(),
    )
    n_x = len({device.coords[0] for device in mesh.devices.flat})
    return jax.shard_map(
        functools.partial(shards, n_x),
        mesh=mesh,
        in_specs=placed,
        out_specs=(P("dom", None), P("dom", None), P("dom", None), P("dom", None)),
        check_vma=False,
    )
```

```python
import functools
import math

import jax
import jax.numpy as jnp
from jax import lax
from jax.sharding import PartitionSpec as P

BLOCK = 128


loss_gain = 16.0
offsets_by = (1, 2, -1, -2)


def passed_along(shard, axis, by):
    count = lax.axis_size(axis)
    return lax.ppermute(shard, axis, [(i, (i + by) % count) for i in range(count)])


def swapped(shard, axis, mask):
    count = lax.axis_size(axis)
    return lax.ppermute(shard, axis, [(i, i ^ mask) for i in range(count)])


def silu_slope(argument):
    sigmoid_v = jax.nn.sigmoid(argument)
    return sigmoid_v * (1.0 + argument * (1.0 - sigmoid_v))


def neighbour_tables(blocks, send_list, patch_blocks):
    n_send = send_list.shape[0]
    width, wide = blocks.shape[2], patch_blocks.shape[2]
    common = max(width, wide)
    outgoing = jnp.concatenate(
        [lax.dynamic_index_in_dim(blocks, send_list[i], 0) for i in range(n_send)], axis=0
    )
    packed = jnp.concatenate(
        [
            jnp.pad(outgoing, ((0, 0), (0, 0), (0, common - width))),
            jnp.pad(patch_blocks, ((0, 0), (0, 0), (0, common - wide))),
        ],
        axis=0,
    )
    block_parts = [blocks]
    patch_parts = [patch_blocks]
    for step_by in offsets_by:
        got = passed_along(packed, "dom", step_by)
        block_parts.append(got[:n_send, :, :width])
        patch_parts.append(got[n_send:, :, :wide])
    return jnp.concatenate(block_parts, axis=0), jnp.concatenate(patch_parts, axis=0)


def logical_pairs(n_y, n_x, axis_is_x, mask):
    pairs = []
    for y in range(n_y):
        for x in range(n_x):
            for c in range(2):
                lx, ly = (x - c) % n_x, (y - c) % n_y
                if axis_is_x:
                    lx ^= mask
                else:
                    ly ^= mask
                px, py = (lx + c) % n_x, (ly + c) % n_y
                pairs.append(((y * n_x + x) * 2 + c, (py * n_x + px) * 2 + c))
    return pairs


def halving_steps(n_y):
    return [("y", b) for b in range(n_y.bit_length() - 1)]


def share_order(rows, n_dom, n_x):
    n_y = n_dom // (2 * n_x)
    per = rows // n_dom
    steps = halving_steps(n_y)
    slots = [None] * n_dom
    for c in range(2):
        for ly in range(n_y):
            for lx in range(n_x):
                d = ((ly + c) % n_y * n_x + (lx + c) % n_x) * 2 + c
                slot = c * n_x + lx
                for _, b in steps:
                    slot = slot * 2 + ((ly >> b) & 1)
                slots[slot] = d
    order = []
    for d in slots:
        order.extend(range(d * per, (d + 1) * per))
    return jnp.array(order, dtype=jnp.int32)


def shifted_x(shard, n_y, n_x, by):
    pairs = []
    for y in range(n_y):
        for x in range(n_x):
            for c in range(2):
                pairs.append(((y * n_x + x) * 2 + c, (y * n_x + (x + by) % n_x) * 2 + c))
    return lax.ppermute(shard, "dom", pairs)


def reduce_to_share(terms, n_dom, n_x):
    bf16 = jnp.bfloat16
    f32 = jnp.float32
    n_y = n_dom // (2 * n_x)
    flat = jnp.concatenate(
        [t[share_order(t.shape[0], n_dom, n_x)].reshape(2, n_y * n_x, -1) for t in terms], axis=2
    )
    width = flat.shape[2]
    me = lax.axis_index("dom")
    core = me % 2
    mine = lax.dynamic_index_in_dim(flat, core, 0, keepdims=False)
    other = lax.dynamic_index_in_dim(flat, 1 - core, 0, keepdims=False)
    held = mine + swapped(other.astype(bf16), "dom", 1).astype(f32)
    lx = (me // 2 % n_x - core) % n_x
    ly = (me // (2 * n_x) - core) % n_y
    held = held.reshape(n_x, -1, width)
    total = lax.dynamic_index_in_dim(held, lx, 0, keepdims=False)
    for by in range(1, n_x):
        block = lax.dynamic_index_in_dim(held, (lx + by) % n_x, 0, keepdims=False)
        total = total + shifted_x(block.astype(bf16), n_y, n_x, by).astype(f32)
    held = total
    for step, (kind, b) in enumerate(halving_steps(n_y)):
        held = held.reshape(2, -1, width)
        mine_bit = (ly >> b) & 1
        mine = lax.dynamic_index_in_dim(held, mine_bit, 0, keepdims=False)
        other = lax.dynamic_index_in_dim(held, 1 - mine_bit, 0, keepdims=False)
        pairs = logical_pairs(n_y, n_x, False, 1 << b)
        if step < 2:
            got = lax.ppermute(other.astype(bf16), "dom", pairs).astype(f32)
        else:
            got = lax.ppermute(other, "dom", pairs)
        held = mine + got
    share = held.reshape(-1)
    n_region = lax.axis_size("region")
    step = 1
    while step < n_region:
        share = share + swapped(share, "region", step)
        step *= 2
    pieces = []
    start = 0
    for t in terms:
        size = t.size // n_dom
        pieces.append(share[start : start + size].reshape(t.shape[0] // n_dom, t.shape[1]))
        start += size
    return pieces


def shards(
    n_x,
    gauges,
    couplings,
    adjacency,
    send_list,
    coverage,
    positive,
    patches,
    message_weight,
    self_weight,
    output_weight,
    patch_weight,
):
    f32 = jnp.float32
    bf16 = jnp.bfloat16
    width = gauges.shape[1]
    wide = patches.shape[1]
    count = couplings.shape[0]
    blocks = gauges.reshape(count, BLOCK, width)
    patch_blocks = patches.reshape(-1, BLOCK, wide)
    block_table, patch_table = neighbour_tables(blocks, send_list, patch_blocks)
    picked = block_table[adjacency]
    message = (
        jnp.einsum("bkij,bkjd->bid", couplings, picked, preferred_element_type=f32)
        .astype(bf16)
        .reshape(-1, width)
    )
    pre_act = jnp.dot(message, message_weight, preferred_element_type=f32) + jnp.dot(
        gauges, self_weight, preferred_element_type=f32
    )
    hidden = (gauges.astype(f32) + jax.nn.silu(pre_act)).astype(bf16)
    queries = jnp.dot(hidden, output_weight, preferred_element_type=f32).astype(bf16)
    table_keys = (
        jnp.dot(patch_table.reshape(-1, wide), patch_weight, preferred_element_type=f32)
        .astype(bf16)
        .reshape(patch_table.shape)
    )
    key_rows = table_keys[coverage].reshape(count, -1, wide)
    flat_cover = patch_table[coverage].reshape(-1, wide)
    query_blocks = queries.reshape(count, BLOCK, wide)
    inv_root = 1.0 / math.sqrt(wide)
    logits = (
        jnp.einsum("bie,bje->bij", query_blocks, key_rows, preferred_element_type=f32) * inv_root
    )
    soft = jax.nn.softmax(logits, axis=-1)
    columns = jnp.arange(logits.shape[2], dtype=jnp.int32)
    target = (positive.reshape(count, BLOCK)[:, :, None] == columns).astype(f32)
    total_gauges = gauges.shape[0] * lax.axis_size("region") * lax.axis_size("dom")
    loss_scale = loss_gain / math.sqrt(total_gauges)
    logit_grad = lax.optimization_barrier(((soft - target) * loss_scale).astype(bf16))
    query_grad = (
        (jnp.einsum("bij,bje->bie", logit_grad, key_rows, preferred_element_type=f32) * inv_root)
        .astype(bf16)
        .reshape(-1, wide)
    )
    key_grad = (
        (
            jnp.einsum("bij,bie->bje", logit_grad, query_blocks, preferred_element_type=f32)
            * inv_root
        )
        .astype(bf16)
        .reshape(-1, wide)
    )
    grad_patch = jnp.dot(flat_cover.T, key_grad, preferred_element_type=f32)
    grad_output = jnp.dot(hidden.T, query_grad, preferred_element_type=f32)
    hidden_grad = jnp.dot(query_grad, output_weight.T, preferred_element_type=f32)
    act_grad = (hidden_grad * silu_slope(pre_act)).astype(bf16)
    grad_message = jnp.dot(message.T, act_grad, preferred_element_type=f32)
    grad_self = jnp.dot(gauges.T, act_grad, preferred_element_type=f32)
    shares = reduce_to_share(
        [grad_message, grad_self, grad_output, grad_patch], lax.axis_size("dom"), n_x
    )
    return tuple(s.astype(bf16) for s in shares)


def solution(mesh):
    placed = (
        P(("region", "dom"), None),
        P(("region", "dom"), None, None, None),
        P(("region", "dom"), None),
        P(("region", "dom")),
        P(("region", "dom"), None),
        P(("region", "dom")),
        P(("region", "dom"), None),
        P(),
        P(),
        P(),
        P(),
    )
    n_x = len({device.coords[0] for device in mesh.devices.flat})
    return jax.shard_map(
        functools.partial(shards, n_x),
        mesh=mesh,
        in_specs=placed,
        out_specs=(P("dom", None), P("dom", None), P("dom", None), P("dom", None)),
        check_vma=False,
    )
```

```python
import functools
import math

import jax
import jax.numpy as jnp
from jax import lax
from jax.sharding import PartitionSpec as P

BLOCK = 128


loss_gain = 16.0
offsets_by = (1, 2, -1, -2)


def passed_along(shard, axis, by):
    count = lax.axis_size(axis)
    return lax.ppermute(shard, axis, [(i, (i + by) % count) for i in range(count)])


def swapped(shard, axis, mask):
    count = lax.axis_size(axis)
    return lax.ppermute(shard, axis, [(i, i ^ mask) for i in range(count)])


def silu_slope(argument):
    sigmoid_v = jax.nn.sigmoid(argument)
    return sigmoid_v * (1.0 + argument * (1.0 - sigmoid_v))


def neighbour_tables(blocks, send_list, patch_blocks):
    outgoing = blocks[send_list]
    n_send = outgoing.shape[0]
    gauge_size = outgoing.size
    packed = jnp.concatenate([outgoing.reshape(-1), patch_blocks.reshape(-1)])
    block_parts = [blocks]
    patch_parts = [patch_blocks]
    for step_by in offsets_by:
        got = passed_along(packed, "dom", step_by)
        block_parts.append(got[:gauge_size].reshape(n_send, BLOCK, blocks.shape[2]))
        patch_parts.append(got[gauge_size:].reshape(patch_blocks.shape))
    return jnp.concatenate(block_parts, axis=0), jnp.concatenate(patch_parts, axis=0)


def logical_pairs(n_y, n_x, axis_is_x, mask):
    pairs = []
    for y in range(n_y):
        for x in range(n_x):
            for c in range(2):
                lx, ly = (x - c) % n_x, (y - c) % n_y
                if axis_is_x:
                    lx ^= mask
                else:
                    ly ^= mask
                px, py = (lx + c) % n_x, (ly + c) % n_y
                pairs.append(((y * n_x + x) * 2 + c, (py * n_x + px) * 2 + c))
    return pairs


def halving_steps(n_y):
    return [("y", b) for b in range(n_y.bit_length() - 1)]


def share_order(rows, n_dom, n_x):
    n_y = n_dom // (2 * n_x)
    per = rows // n_dom
    steps = halving_steps(n_y)
    slots = [None] * n_dom
    for c in range(2):
        for ly in range(n_y):
            for lx in range(n_x):
                d = ((ly + c) % n_y * n_x + (lx + c) % n_x) * 2 + c
                slot = c * n_x + lx
                for _, b in steps:
                    slot = slot * 2 + ((ly >> b) & 1)
                slots[slot] = d
    order = []
    for d in slots:
        order.extend(range(d * per, (d + 1) * per))
    return jnp.array(order, dtype=jnp.int32)


def shifted_x(shard, n_y, n_x, by):
    pairs = []
    for y in range(n_y):
        for x in range(n_x):
            for c in range(2):
                pairs.append(((y * n_x + x) * 2 + c, (y * n_x + (x + by) % n_x) * 2 + c))
    return lax.ppermute(shard, "dom", pairs)


def reduce_to_share(terms, n_dom, n_x):
    bf16 = jnp.bfloat16
    f32 = jnp.float32
    n_y = n_dom // (2 * n_x)
    by_dest = jnp.concatenate([t.reshape(n_dom, -1) for t in terms], axis=1)
    flat = by_dest[share_order(n_dom, n_dom, n_x)].reshape(2, n_y * n_x, -1)
    width = flat.shape[2]
    me = lax.axis_index("dom")
    core = me % 2
    mine = lax.dynamic_index_in_dim(flat, core, 0, keepdims=False)
    other = lax.dynamic_index_in_dim(flat, 1 - core, 0, keepdims=False)
    held = mine + swapped(other.astype(bf16), "dom", 1).astype(f32)
    lx = (me // 2 % n_x - core) % n_x
    ly = (me // (2 * n_x) - core) % n_y
    held = held.reshape(n_x, -1, width)
    total = lax.dynamic_index_in_dim(held, lx, 0, keepdims=False)
    for by in range(1, n_x):
        block = lax.dynamic_index_in_dim(held, (lx + by) % n_x, 0, keepdims=False)
        total = total + shifted_x(block.astype(bf16), n_y, n_x, by).astype(f32)
    held = total
    for step, (kind, b) in enumerate(halving_steps(n_y)):
        held = held.reshape(2, -1, width)
        mine_bit = (ly >> b) & 1
        mine = lax.dynamic_index_in_dim(held, mine_bit, 0, keepdims=False)
        other = lax.dynamic_index_in_dim(held, 1 - mine_bit, 0, keepdims=False)
        pairs = logical_pairs(n_y, n_x, False, 1 << b)
        if step < 2:
            got = lax.ppermute(other.astype(bf16), "dom", pairs).astype(f32)
        else:
            got = lax.ppermute(other, "dom", pairs)
        held = mine + got
    share = held.reshape(-1)
    n_region = lax.axis_size("region")
    step = 1
    while step < n_region:
        share = share + swapped(share, "region", step)
        step *= 2
    pieces = []
    start = 0
    for t in terms:
        size = t.size // n_dom
        pieces.append(share[start : start + size].reshape(t.shape[0] // n_dom, t.shape[1]))
        start += size
    return pieces


def shards(
    n_x,
    gauges,
    couplings,
    adjacency,
    send_list,
    coverage,
    positive,
    patches,
    message_weight,
    self_weight,
    output_weight,
    patch_weight,
):
    f32 = jnp.float32
    bf16 = jnp.bfloat16
    width = gauges.shape[1]
    wide = patches.shape[1]
    count = couplings.shape[0]
    blocks = gauges.reshape(count, BLOCK, width)
    patch_blocks = patches.reshape(-1, BLOCK, wide)
    block_table, patch_table = neighbour_tables(blocks, send_list, patch_blocks)
    picked = block_table[adjacency]
    message = (
        jnp.einsum("bkij,bkjd->bid", couplings, picked, preferred_element_type=f32)
        .astype(bf16)
        .reshape(-1, width)
    )
    pre_act = jnp.dot(message, message_weight, preferred_element_type=f32) + jnp.dot(
        gauges, self_weight, preferred_element_type=f32
    )
    hidden = (gauges.astype(f32) + jax.nn.silu(pre_act)).astype(bf16)
    queries = jnp.dot(hidden, output_weight, preferred_element_type=f32).astype(bf16)
    table_keys = (
        jnp.dot(patch_table.reshape(-1, wide), patch_weight, preferred_element_type=f32)
        .astype(bf16)
        .reshape(patch_table.shape)
    )
    key_rows = table_keys[coverage].reshape(count, -1, wide)
    flat_cover = patch_table[coverage].reshape(-1, wide)
    query_blocks = queries.reshape(count, BLOCK, wide)
    inv_root = 1.0 / math.sqrt(wide)
    logits = (
        jnp.einsum("bie,bje->bij", query_blocks, key_rows, preferred_element_type=f32) * inv_root
    )
    soft = jax.nn.softmax(logits, axis=-1)
    columns = jnp.arange(logits.shape[2], dtype=jnp.int32)
    target = (positive.reshape(count, BLOCK)[:, :, None] == columns).astype(f32)
    total_gauges = gauges.shape[0] * lax.axis_size("region") * lax.axis_size("dom")
    loss_scale = loss_gain / math.sqrt(total_gauges)
    logit_grad = lax.optimization_barrier(((soft - target) * loss_scale).astype(bf16))
    query_grad = (
        (jnp.einsum("bij,bje->bie", logit_grad, key_rows, preferred_element_type=f32) * inv_root)
        .astype(bf16)
        .reshape(-1, wide)
    )
    key_grad = (
        (
            jnp.einsum("bij,bie->bje", logit_grad, query_blocks, preferred_element_type=f32)
            * inv_root
        )
        .astype(bf16)
        .reshape(-1, wide)
    )
    grad_patch = jnp.dot(flat_cover.T, key_grad, preferred_element_type=f32)
    grad_output = jnp.dot(hidden.T, query_grad, preferred_element_type=f32)
    hidden_grad = jnp.dot(query_grad, output_weight.T, preferred_element_type=f32)
    act_grad = (hidden_grad * silu_slope(pre_act)).astype(bf16)
    grad_message = jnp.dot(message.T, act_grad, preferred_element_type=f32)
    grad_self = jnp.dot(gauges.T, act_grad, preferred_element_type=f32)
    shares = reduce_to_share(
        [grad_message, grad_self, grad_output, grad_patch], lax.axis_size("dom"), n_x
    )
    return tuple(s.astype(bf16) for s in shares)


def solution(mesh):
    placed = (
        P(("region", "dom"), None),
        P(("region", "dom"), None, None, None),
        P(("region", "dom"), None),
        P(("region", "dom")),
        P(("region", "dom"), None),
        P(("region", "dom")),
        P(("region", "dom"), None),
        P(),
        P(),
        P(),
        P(),
    )
    n_x = len({device.coords[0] for device in mesh.devices.flat})
    return jax.shard_map(
        functools.partial(shards, n_x),
        mesh=mesh,
        in_specs=placed,
        out_specs=(P("dom", None), P("dom", None), P("dom", None), P("dom", None)),
        check_vma=False,
    )
```

```python
import functools
import math

import jax
import jax.numpy as jnp
from jax import lax
from jax.sharding import PartitionSpec as P

BLOCK = 128


loss_gain = 16.0
offsets_by = (1, 2, -1, -2)


def passed_along(shard, axis, by):
    count = lax.axis_size(axis)
    return lax.ppermute(shard, axis, [(i, (i + by) % count) for i in range(count)])


def swapped(shard, axis, mask):
    count = lax.axis_size(axis)
    return lax.ppermute(shard, axis, [(i, i ^ mask) for i in range(count)])


def silu_slope(argument):
    sigmoid_v = jax.nn.sigmoid(argument)
    return sigmoid_v * (1.0 + argument * (1.0 - sigmoid_v))


def neighbour_tables(blocks, send_list, patch_blocks):
    outgoing = blocks[send_list]
    n_send = outgoing.shape[0]
    gauge_size = outgoing.size
    packed = jnp.concatenate([outgoing.reshape(-1), patch_blocks.reshape(-1)])
    block_parts = [blocks]
    patch_parts = [patch_blocks]
    for step_by in offsets_by:
        got = passed_along(packed, "dom", step_by)
        block_parts.append(got[:gauge_size].reshape(n_send, BLOCK, blocks.shape[2]))
        patch_parts.append(got[gauge_size:].reshape(patch_blocks.shape))
    return jnp.concatenate(block_parts, axis=0), jnp.concatenate(patch_parts, axis=0)


def logical_pairs(n_y, n_x, axis_is_x, mask):
    pairs = []
    for y in range(n_y):
        for x in range(n_x):
            for c in range(2):
                lx, ly = (x - c) % n_x, (y - c) % n_y
                if axis_is_x:
                    lx ^= mask
                else:
                    ly ^= mask
                px, py = (lx + c) % n_x, (ly + c) % n_y
                pairs.append(((y * n_x + x) * 2 + c, (py * n_x + px) * 2 + c))
    return pairs


def halving_steps(n_y):
    return [("y", b) for b in range(n_y.bit_length() - 1)]


def share_order(rows, n_dom, n_x):
    n_y = n_dom // (2 * n_x)
    per = rows // n_dom
    steps = halving_steps(n_y)
    slots = [None] * n_dom
    for c in range(2):
        for ly in range(n_y):
            for lx in range(n_x):
                d = ((ly + c) % n_y * n_x + (lx + c) % n_x) * 2 + c
                slot = c * n_x + lx
                for _, b in steps:
                    slot = slot * 2 + ((ly >> b) & 1)
                slots[slot] = d
    order = []
    for d in slots:
        order.extend(range(d * per, (d + 1) * per))
    return jnp.array(order, dtype=jnp.int32)


def shifted_x(shard, n_y, n_x, by):
    pairs = []
    for y in range(n_y):
        for x in range(n_x):
            for c in range(2):
                pairs.append(((y * n_x + x) * 2 + c, (y * n_x + (x + by) % n_x) * 2 + c))
    return lax.ppermute(shard, "dom", pairs)


def reduce_to_share(terms, n_dom, n_x):
    bf16 = jnp.bfloat16
    f32 = jnp.float32
    n_y = n_dom // (2 * n_x)
    flat = jnp.concatenate(
        [t[share_order(t.shape[0], n_dom, n_x)].reshape(2, n_y * n_x, -1) for t in terms], axis=2
    )
    width = flat.shape[2]
    me = lax.axis_index("dom")
    core = me % 2
    mine = lax.dynamic_index_in_dim(flat, core, 0, keepdims=False)
    other = lax.dynamic_index_in_dim(flat, 1 - core, 0, keepdims=False)
    held = mine + swapped(other.astype(bf16), "dom", 1).astype(f32)
    lx = (me // 2 % n_x - core) % n_x
    ly = (me // (2 * n_x) - core) % n_y
    held = held.reshape(n_x, -1, width)
    total = lax.dynamic_index_in_dim(held, lx, 0, keepdims=False)
    for by in range(1, n_x):
        block = lax.dynamic_index_in_dim(held, (lx + by) % n_x, 0, keepdims=False)
        total = total + shifted_x(block.astype(bf16), n_y, n_x, by).astype(f32)
    held = total
    for step, (kind, b) in enumerate(halving_steps(n_y)):
        held = held.reshape(2, -1, width)
        mine_bit = (ly >> b) & 1
        mine = lax.dynamic_index_in_dim(held, mine_bit, 0, keepdims=False)
        other = lax.dynamic_index_in_dim(held, 1 - mine_bit, 0, keepdims=False)
        pairs = logical_pairs(n_y, n_x, False, 1 << b)
        if step < 2:
            got = lax.ppermute(other.astype(bf16), "dom", pairs).astype(f32)
        else:
            got = lax.ppermute(other, "dom", pairs)
        held = mine + got
    share = held.reshape(-1)
    n_region = lax.axis_size("region")
    step = n_region // 2
    while step >= 1:
        share = share + swapped(share, "region", step)
        step //= 2
    pieces = []
    start = 0
    for t in terms:
        size = t.size // n_dom
        pieces.append(share[start : start + size].reshape(t.shape[0] // n_dom, t.shape[1]))
        start += size
    return pieces


def shards(
    n_x,
    gauges,
    couplings,
    adjacency,
    send_list,
    coverage,
    positive,
    patches,
    message_weight,
    self_weight,
    output_weight,
    patch_weight,
):
    f32 = jnp.float32
    bf16 = jnp.bfloat16
    width = gauges.shape[1]
    wide = patches.shape[1]
    count = couplings.shape[0]
    blocks = gauges.reshape(count, BLOCK, width)
    patch_blocks = patches.reshape(-1, BLOCK, wide)
    block_table, patch_table = neighbour_tables(blocks, send_list, patch_blocks)
    picked = block_table[adjacency]
    message = (
        jnp.einsum("bkij,bkjd->bid", couplings, picked, preferred_element_type=f32)
        .astype(bf16)
        .reshape(-1, width)
    )
    pre_act = jnp.dot(message, message_weight, preferred_element_type=f32) + jnp.dot(
        gauges, self_weight, preferred_element_type=f32
    )
    hidden = (gauges.astype(f32) + jax.nn.silu(pre_act)).astype(bf16)
    queries = jnp.dot(hidden, output_weight, preferred_element_type=f32).astype(bf16)
    table_keys = (
        jnp.dot(patch_table.reshape(-1, wide), patch_weight, preferred_element_type=f32)
        .astype(bf16)
        .reshape(patch_table.shape)
    )
    key_rows = table_keys[coverage].reshape(count, -1, wide)
    flat_cover = patch_table[coverage].reshape(-1, wide)
    query_blocks = queries.reshape(count, BLOCK, wide)
    inv_root = 1.0 / math.sqrt(wide)
    logits = (
        jnp.einsum("bie,bje->bij", query_blocks, key_rows, preferred_element_type=f32) * inv_root
    )
    soft = jax.nn.softmax(logits, axis=-1)
    columns = jnp.arange(logits.shape[2], dtype=jnp.int32)
    target = (positive.reshape(count, BLOCK)[:, :, None] == columns).astype(f32)
    total_gauges = gauges.shape[0] * lax.axis_size("region") * lax.axis_size("dom")
    loss_scale = loss_gain / math.sqrt(total_gauges)
    logit_grad = lax.optimization_barrier(((soft - target) * loss_scale).astype(bf16))
    query_grad = (
        (jnp.einsum("bij,bje->bie", logit_grad, key_rows, preferred_element_type=f32) * inv_root)
        .astype(bf16)
        .reshape(-1, wide)
    )
    key_grad = (
        (
            jnp.einsum("bij,bie->bje", logit_grad, query_blocks, preferred_element_type=f32)
            * inv_root
        )
        .astype(bf16)
        .reshape(-1, wide)
    )
    grad_patch = jnp.dot(flat_cover.T, key_grad, preferred_element_type=f32)
    grad_output = jnp.dot(hidden.T, query_grad, preferred_element_type=f32)
    hidden_grad = jnp.dot(query_grad, output_weight.T, preferred_element_type=f32)
    act_grad = (hidden_grad * silu_slope(pre_act)).astype(bf16)
    grad_message = jnp.dot(message.T, act_grad, preferred_element_type=f32)
    grad_self = jnp.dot(gauges.T, act_grad, preferred_element_type=f32)
    shares = reduce_to_share(
        [grad_message, grad_self, grad_output, grad_patch], lax.axis_size("dom"), n_x
    )
    return tuple(s.astype(bf16) for s in shares)


def solution(mesh):
    placed = (
        P(("region", "dom"), None),
        P(("region", "dom"), None, None, None),
        P(("region", "dom"), None),
        P(("region", "dom")),
        P(("region", "dom"), None),
        P(("region", "dom")),
        P(("region", "dom"), None),
        P(),
        P(),
        P(),
        P(),
    )
    n_x = len({device.coords[0] for device in mesh.devices.flat})
    return jax.shard_map(
        functools.partial(shards, n_x),
        mesh=mesh,
        in_specs=placed,
        out_specs=(P("dom", None), P("dom", None), P("dom", None), P("dom", None)),
        check_vma=False,
    )
```

```python
import functools
import math

import jax
import jax.numpy as jnp
from jax import lax
from jax.sharding import PartitionSpec as P

BLOCK = 128


loss_gain = 16.0
offsets_by = (1, 2, -1, -2)


def passed_along(shard, axis, by):
    count = lax.axis_size(axis)
    return lax.ppermute(shard, axis, [(i, (i + by) % count) for i in range(count)])


def swapped(shard, axis, mask):
    count = lax.axis_size(axis)
    return lax.ppermute(shard, axis, [(i, i ^ mask) for i in range(count)])


def silu_slope(argument):
    sigmoid_v = jax.nn.sigmoid(argument)
    return sigmoid_v * (1.0 + argument * (1.0 - sigmoid_v))


def neighbour_tables(blocks, send_list, patch_blocks):
    outgoing = blocks[send_list]
    n_send = outgoing.shape[0]
    gauge_size = outgoing.size
    packed = jnp.concatenate([outgoing.reshape(-1), patch_blocks.reshape(-1)])
    block_parts = [blocks]
    patch_parts = [patch_blocks]
    for step_by in offsets_by:
        got = passed_along(packed, "dom", step_by)
        block_parts.append(got[:gauge_size].reshape(n_send, BLOCK, blocks.shape[2]))
        patch_parts.append(got[gauge_size:].reshape(patch_blocks.shape))
    return jnp.concatenate(block_parts, axis=0), jnp.concatenate(patch_parts, axis=0)


def logical_pairs(n_y, n_x, axis_is_x, mask):
    pairs = []
    for y in range(n_y):
        for x in range(n_x):
            for c in range(2):
                lx, ly = (x - c) % n_x, (y - c) % n_y
                if axis_is_x:
                    lx ^= mask
                else:
                    ly ^= mask
                px, py = (lx + c) % n_x, (ly + c) % n_y
                pairs.append(((y * n_x + x) * 2 + c, (py * n_x + px) * 2 + c))
    return pairs


def halving_steps(n_y):
    return [("y", b) for b in range(n_y.bit_length() - 1)]


def share_order(rows, n_dom, n_x):
    n_y = n_dom // (2 * n_x)
    per = rows // n_dom
    steps = halving_steps(n_y)
    slots = [None] * n_dom
    for c in range(2):
        for ly in range(n_y):
            for lx in range(n_x):
                d = ((ly + c) % n_y * n_x + (lx + c) % n_x) * 2 + c
                slot = c * n_x + lx
                for _, b in steps:
                    slot = slot * 2 + ((ly >> b) & 1)
                slots[slot] = d
    order = []
    for d in slots:
        order.extend(range(d * per, (d + 1) * per))
    return jnp.array(order, dtype=jnp.int32)


def shifted_x(shard, n_y, n_x, by):
    pairs = []
    for y in range(n_y):
        for x in range(n_x):
            for c in range(2):
                pairs.append(((y * n_x + x) * 2 + c, (y * n_x + (x + by) % n_x) * 2 + c))
    return lax.ppermute(shard, "dom", pairs)


def reduce_to_share(terms, n_dom, n_x):
    bf16 = jnp.bfloat16
    f32 = jnp.float32
    n_y = n_dom // (2 * n_x)
    flat = jnp.concatenate(
        [t[share_order(t.shape[0], n_dom, n_x)].reshape(2, n_y * n_x, -1) for t in terms], axis=2
    )
    width = flat.shape[2]
    me = lax.axis_index("dom")
    core = me % 2
    mine = lax.dynamic_index_in_dim(flat, core, 0, keepdims=False)
    other = lax.dynamic_index_in_dim(flat, 1 - core, 0, keepdims=False)
    held = mine + swapped(other.astype(bf16), "dom", 1).astype(f32)
    lx = (me // 2 % n_x - core) % n_x
    ly = (me // (2 * n_x) - core) % n_y
    held = held.reshape(n_x, -1, width)
    total = lax.dynamic_index_in_dim(held, lx, 0, keepdims=False)
    for by in range(1, n_x):
        block = lax.dynamic_index_in_dim(held, (lx + by) % n_x, 0, keepdims=False)
        total = total + shifted_x(block.astype(bf16), n_y, n_x, by).astype(f32)
    held = total
    for step, (kind, b) in enumerate(halving_steps(n_y)):
        held = held.reshape(2, -1, width)
        mine_bit = (ly >> b) & 1
        mine = lax.dynamic_index_in_dim(held, mine_bit, 0, keepdims=False)
        other = lax.dynamic_index_in_dim(held, 1 - mine_bit, 0, keepdims=False)
        pairs = logical_pairs(n_y, n_x, False, 1 << b)
        if step < 2:
            got = lax.ppermute(other.astype(bf16), "dom", pairs).astype(f32)
        else:
            got = lax.ppermute(other, "dom", pairs)
        held = mine + got
    share = held.reshape(-1)
    n_region = lax.axis_size("region")
    step = n_region // 2
    while step >= 1:
        share = share + swapped(share, "region", step)
        step //= 2
    pieces = []
    start = 0
    for t in terms:
        size = t.size // n_dom
        pieces.append(share[start : start + size].reshape(t.shape[0] // n_dom, t.shape[1]))
        start += size
    return pieces


def shards(
    n_x,
    gauges,
    couplings,
    adjacency,
    send_list,
    coverage,
    positive,
    patches,
    message_weight,
    self_weight,
    output_weight,
    patch_weight,
):
    f32 = jnp.float32
    bf16 = jnp.bfloat16
    width = gauges.shape[1]
    wide = patches.shape[1]
    count = couplings.shape[0]
    blocks = gauges.reshape(count, BLOCK, width)
    patch_blocks = patches.reshape(-1, BLOCK, wide)
    self_part = lax.optimization_barrier(jnp.dot(gauges, self_weight, preferred_element_type=f32))
    block_table, patch_table = neighbour_tables(blocks, send_list, patch_blocks)
    picked = block_table[adjacency]
    message = (
        jnp.einsum("bkij,bkjd->bid", couplings, picked, preferred_element_type=f32)
        .astype(bf16)
        .reshape(-1, width)
    )
    pre_act = jnp.dot(message, message_weight, preferred_element_type=f32) + self_part
    hidden = (gauges.astype(f32) + jax.nn.silu(pre_act)).astype(bf16)
    queries = jnp.dot(hidden, output_weight, preferred_element_type=f32).astype(bf16)
    table_keys = (
        jnp.dot(patch_table.reshape(-1, wide), patch_weight, preferred_element_type=f32)
        .astype(bf16)
        .reshape(patch_table.shape)
    )
    key_rows = table_keys[coverage].reshape(count, -1, wide)
    flat_cover = patch_table[coverage].reshape(-1, wide)
    query_blocks = queries.reshape(count, BLOCK, wide)
    inv_root = 1.0 / math.sqrt(wide)
    logits = (
        jnp.einsum("bie,bje->bij", query_blocks, key_rows, preferred_element_type=f32) * inv_root
    )
    soft = jax.nn.softmax(logits, axis=-1)
    columns = jnp.arange(logits.shape[2], dtype=jnp.int32)
    target = (positive.reshape(count, BLOCK)[:, :, None] == columns).astype(f32)
    total_gauges = gauges.shape[0] * lax.axis_size("region") * lax.axis_size("dom")
    loss_scale = loss_gain / math.sqrt(total_gauges)
    logit_grad = lax.optimization_barrier(((soft - target) * loss_scale).astype(bf16))
    query_grad = (
        (jnp.einsum("bij,bje->bie", logit_grad, key_rows, preferred_element_type=f32) * inv_root)
        .astype(bf16)
        .reshape(-1, wide)
    )
    key_grad = (
        (
            jnp.einsum("bij,bie->bje", logit_grad, query_blocks, preferred_element_type=f32)
            * inv_root
        )
        .astype(bf16)
        .reshape(-1, wide)
    )
    grad_patch = jnp.dot(flat_cover.T, key_grad, preferred_element_type=f32)
    grad_output = jnp.dot(hidden.T, query_grad, preferred_element_type=f32)
    hidden_grad = jnp.dot(query_grad, output_weight.T, preferred_element_type=f32)
    act_grad = (hidden_grad * silu_slope(pre_act)).astype(bf16)
    grad_message = jnp.dot(message.T, act_grad, preferred_element_type=f32)
    grad_self = jnp.dot(gauges.T, act_grad, preferred_element_type=f32)
    shares = reduce_to_share(
        [grad_message, grad_self, grad_output, grad_patch], lax.axis_size("dom"), n_x
    )
    return tuple(s.astype(bf16) for s in shares)


def solution(mesh):
    placed = (
        P(("region", "dom"), None),
        P(("region", "dom"), None, None, None),
        P(("region", "dom"), None),
        P(("region", "dom")),
        P(("region", "dom"), None),
        P(("region", "dom")),
        P(("region", "dom"), None),
        P(),
        P(),
        P(),
        P(),
    )
    n_x = len({device.coords[0] for device in mesh.devices.flat})
    return jax.shard_map(
        functools.partial(shards, n_x),
        mesh=mesh,
        in_specs=placed,
        out_specs=(P("dom", None), P("dom", None), P("dom", None), P("dom", None)),
        check_vma=False,
    )
```

```python
import functools
import math

import jax
import jax.numpy as jnp
from jax import lax
from jax.sharding import PartitionSpec as P

BLOCK = 128


loss_gain = 16.0
offsets_by = (1, 2, -1, -2)


def passed_along(shard, axis, by):
    count = lax.axis_size(axis)
    return lax.ppermute(shard, axis, [(i, (i + by) % count) for i in range(count)])


def swapped(shard, axis, mask):
    count = lax.axis_size(axis)
    return lax.ppermute(shard, axis, [(i, i ^ mask) for i in range(count)])


def silu_slope(argument):
    sigmoid_v = jax.nn.sigmoid(argument)
    return sigmoid_v * (1.0 + argument * (1.0 - sigmoid_v))


def neighbour_tables(blocks, send_list, patch_blocks):
    outgoing = blocks[send_list]
    n_send = outgoing.shape[0]
    gauge_size = outgoing.size
    packed = jnp.concatenate([outgoing.reshape(-1), patch_blocks.reshape(-1)])
    block_parts = [blocks]
    patch_parts = [patch_blocks]
    for step_by in offsets_by:
        got = passed_along(packed, "dom", step_by)
        block_parts.append(got[:gauge_size].reshape(n_send, BLOCK, blocks.shape[2]))
        patch_parts.append(got[gauge_size:].reshape(patch_blocks.shape))
    return jnp.concatenate(block_parts, axis=0), jnp.concatenate(patch_parts, axis=0)


def logical_pairs(n_y, n_x, axis_is_x, mask):
    pairs = []
    for y in range(n_y):
        for x in range(n_x):
            for c in range(2):
                lx, ly = (x - c) % n_x, (y - c) % n_y
                if axis_is_x:
                    lx ^= mask
                else:
                    ly ^= mask
                px, py = (lx + c) % n_x, (ly + c) % n_y
                pairs.append(((y * n_x + x) * 2 + c, (py * n_x + px) * 2 + c))
    return pairs


def halving_steps(n_y):
    return [("y", b) for b in range(n_y.bit_length() - 1)]


def share_order(rows, n_dom, n_x):
    n_y = n_dom // (2 * n_x)
    per = rows // n_dom
    steps = halving_steps(n_y)
    slots = [None] * n_dom
    for c in range(2):
        for ly in range(n_y):
            for lx in range(n_x):
                d = ((ly + c) % n_y * n_x + (lx + c) % n_x) * 2 + c
                slot = c * n_x + lx
                for _, b in steps:
                    slot = slot * 2 + ((ly >> b) & 1)
                slots[slot] = d
    order = []
    for d in slots:
        order.extend(range(d * per, (d + 1) * per))
    return jnp.array(order, dtype=jnp.int32)


def shifted_x(shard, n_y, n_x, by):
    pairs = []
    for y in range(n_y):
        for x in range(n_x):
            for c in range(2):
                pairs.append(((y * n_x + x) * 2 + c, (y * n_x + (x + by) % n_x) * 2 + c))
    return lax.ppermute(shard, "dom", pairs)


def reduce_to_share(terms, n_dom, n_x):
    bf16 = jnp.bfloat16
    f32 = jnp.float32
    n_y = n_dom // (2 * n_x)
    flat = jnp.concatenate(
        [t[share_order(t.shape[0], n_dom, n_x)].reshape(2, n_y * n_x, -1) for t in terms], axis=2
    )
    width = flat.shape[2]
    me = lax.axis_index("dom")
    core = me % 2
    mine = lax.dynamic_index_in_dim(flat, core, 0, keepdims=False)
    other = lax.dynamic_index_in_dim(flat, 1 - core, 0, keepdims=False)
    held = mine + swapped(other.astype(bf16), "dom", 1).astype(f32)
    lx = (me // 2 % n_x - core) % n_x
    ly = (me // (2 * n_x) - core) % n_y
    held = held.reshape(n_x, -1, width)
    total = lax.dynamic_index_in_dim(held, lx, 0, keepdims=False)
    for by in range(1, n_x):
        block = lax.dynamic_index_in_dim(held, (lx + by) % n_x, 0, keepdims=False)
        total = total + shifted_x(block.astype(bf16), n_y, n_x, by).astype(f32)
    held = total
    for step, (kind, b) in enumerate(halving_steps(n_y)):
        held = held.reshape(2, -1, width)
        mine_bit = (ly >> b) & 1
        mine = lax.dynamic_index_in_dim(held, mine_bit, 0, keepdims=False)
        other = lax.dynamic_index_in_dim(held, 1 - mine_bit, 0, keepdims=False)
        pairs = logical_pairs(n_y, n_x, False, 1 << b)
        if step < 2:
            got = lax.ppermute(other.astype(bf16), "dom", pairs).astype(f32)
        else:
            got = lax.ppermute(other, "dom", pairs)
        held = mine + got
    share = held.reshape(-1)
    n_region = lax.axis_size("region")
    step = n_region // 2
    while step > 1:
        share = share + swapped(share, "region", step)
        step //= 2
    partner = swapped(share, "region", 1)
    pieces = []
    start = 0
    for t in terms:
        size = t.size // n_dom
        piece = share[start : start + size] + partner[start : start + size]
        pieces.append(piece.astype(bf16).reshape(t.shape[0] // n_dom, t.shape[1]))
        start += size
    return pieces


def shards(
    n_x,
    gauges,
    couplings,
    adjacency,
    send_list,
    coverage,
    positive,
    patches,
    message_weight,
    self_weight,
    output_weight,
    patch_weight,
):
    f32 = jnp.float32
    bf16 = jnp.bfloat16
    width = gauges.shape[1]
    wide = patches.shape[1]
    count = couplings.shape[0]
    blocks = gauges.reshape(count, BLOCK, width)
    patch_blocks = patches.reshape(-1, BLOCK, wide)
    self_part = lax.optimization_barrier(jnp.dot(gauges, self_weight, preferred_element_type=f32))
    block_table, patch_table = neighbour_tables(blocks, send_list, patch_blocks)
    picked = block_table[adjacency]
    message = (
        jnp.einsum("bkij,bkjd->bid", couplings, picked, preferred_element_type=f32)
        .astype(bf16)
        .reshape(-1, width)
    )
    pre_act = jnp.dot(message, message_weight, preferred_element_type=f32) + self_part
    hidden = (gauges.astype(f32) + jax.nn.silu(pre_act)).astype(bf16)
    queries = jnp.dot(hidden, output_weight, preferred_element_type=f32).astype(bf16)
    table_keys = (
        jnp.dot(patch_table.reshape(-1, wide), patch_weight, preferred_element_type=f32)
        .astype(bf16)
        .reshape(patch_table.shape)
    )
    key_rows = table_keys[coverage].reshape(count, -1, wide)
    flat_cover = patch_table[coverage].reshape(-1, wide)
    query_blocks = queries.reshape(count, BLOCK, wide)
    inv_root = 1.0 / math.sqrt(wide)
    logits = (
        jnp.einsum("bie,bje->bij", query_blocks, key_rows, preferred_element_type=f32) * inv_root
    )
    soft = jax.nn.softmax(logits, axis=-1)
    columns = jnp.arange(logits.shape[2], dtype=jnp.int32)
    target = (positive.reshape(count, BLOCK)[:, :, None] == columns).astype(f32)
    total_gauges = gauges.shape[0] * lax.axis_size("region") * lax.axis_size("dom")
    loss_scale = loss_gain / math.sqrt(total_gauges)
    logit_grad = lax.optimization_barrier(((soft - target) * loss_scale).astype(bf16))
    query_grad = (
        (jnp.einsum("bij,bje->bie", logit_grad, key_rows, preferred_element_type=f32) * inv_root)
        .astype(bf16)
        .reshape(-1, wide)
    )
    key_grad = (
        (
            jnp.einsum("bij,bie->bje", logit_grad, query_blocks, preferred_element_type=f32)
            * inv_root
        )
        .astype(bf16)
        .reshape(-1, wide)
    )
    grad_patch = jnp.dot(flat_cover.T, key_grad, preferred_element_type=f32)
    grad_output = jnp.dot(hidden.T, query_grad, preferred_element_type=f32)
    hidden_grad = jnp.dot(query_grad, output_weight.T, preferred_element_type=f32)
    act_grad = (hidden_grad * silu_slope(pre_act)).astype(bf16)
    grad_message = jnp.dot(message.T, act_grad, preferred_element_type=f32)
    grad_self = jnp.dot(gauges.T, act_grad, preferred_element_type=f32)
    shares = reduce_to_share(
        [grad_message, grad_self, grad_output, grad_patch], lax.axis_size("dom"), n_x
    )
    return tuple(shares)


def solution(mesh):
    placed = (
        P(("region", "dom"), None),
        P(("region", "dom"), None, None, None),
        P(("region", "dom"), None),
        P(("region", "dom")),
        P(("region", "dom"), None),
        P(("region", "dom")),
        P(("region", "dom"), None),
        P(),
        P(),
        P(),
        P(),
    )
    n_x = len({device.coords[0] for device in mesh.devices.flat})
    return jax.shard_map(
        functools.partial(shards, n_x),
        mesh=mesh,
        in_specs=placed,
        out_specs=(P("dom", None), P("dom", None), P("dom", None), P("dom", None)),
        check_vma=False,
    )
```
